256 devices in a mesh: wide: 64 (over z, y, core), narrow: 4 (over x).
Axes of the slice: x: 4, y: 4, z: 8, core: 2. Of those that a mesh axis runs over, the one named last changes fastest.
Arguments:
- file_lengths: int32 [17], replicated, may hold values from 1 to 8, as said below
- queries: bfloat16 [32768, 4096], P('wide', 'narrow'), may hold values from -6 to 6
- out_grad: bfloat16 [32768, 4096], P('wide', 'narrow'), may hold values from -6 to 6
- mem_key: bfloat16 [8192, 1024], P('wide', 'narrow'), may hold values from -6 to 6
- memory_values: bfloat16 [8192, 1024], P('wide', 'narrow'), may hold values from -6 to 6
- enc_rows: bfloat16 [8192, 4096], P('wide'), may hold values from -16 to 16
- key_down: bfloat16 [4096, 128], replicated, may hold values from -0.09375 to 0.09375
- key_up: bfloat16 [128, 1024], P(None, 'narrow'), may hold values from -0.5 to 0.5
- value_down: bfloat16 [4096, 128], replicated, may hold values from -0.09375 to 0.09375
- value_up: bfloat16 [128, 1024], P(None, 'narrow'), may hold values from -0.5 to 0.5
Outputs:
- grad_key_down: float32 [4096, 128], P('wide')
- grad_value_down: float32 [4096, 128], P('wide')
- grad_key_up: float32 [128, 1024], P(None, 'narrow')
- grad_value_up: float32 [128, 1024], P(None, 'narrow')
The draws below stay inside these ranges and needn't reach their ends.
Inputs may be any that keep to these rules, and one draw needn't show every extreme that they name: `file_lengths`: the lengths sum to 64; the last file has 8 stretches.
All inputs are finite; a program needn't handle non-finite values.
Results may differ from the reference program's by a relative error of at most 0.0056.
Values may be sent and summed in bfloat16 or wider, within the bound.
No kernel may reach another device: no remote copies, remote signals or barrier semaphores. Data moves between devices by JAX's collectives and lax.ppermute only.
A program may use at most 128 MiB of HBM per device.

```python
import jax
import jax.numpy as jnp
from jax import lax

D = 4096
HEAD_SIZE = 128
KEY_VALUE_HEADS = 8
Q_PER_KV = 4
LR = 128
QC = 512
MEMORY_ROWS = 128
STRETCH_TOTAL = 64
MAX_STRETCHES = 8
FILES = 17


def compose(key, total, parts, most):
    sizes = jnp.ones((parts,), jnp.int32)
    labels = jnp.arange(parts, dtype=jnp.int32)

    def step(turn, carry):
        current, state = carry
        state, sub = jax.random.split(state)
        score = jax.random.randint(sub, (parts,), 0, 1 << 20) * parts + labels
        score = jnp.where(current < most, score, -1)
        chosen = jnp.argmax(score).astype(jnp.int32)
        current = current + (labels == chosen).astype(jnp.int32)
        return (current, state)
    sizes, unused = lax.fori_loop(0, total - parts, step, (sizes, key))
    return sizes


def draw_file_lengths(key, part):
    most = MAX_STRETCHES
    before = STRETCH_TOTAL - most
    front = compose(jax.random.fold_in(key, 11), before, FILES - 1, most)
    return jnp.concatenate([front, jnp.full((1,), most, jnp.int32)], 0)


def with_spikes(result, stream_key, source, target, shards_of, factor):
    owner, partner = [(jnp.arange(result.shape[dim]) // (result.shape[dim] // shards_of)).reshape([-1 if axis == dim else 1 for axis in range(result.ndim)]) for dim in (source, target)]
    chosen = jax.random.permutation(stream_key, shards_of)[partner]
    strong = (owner == chosen) | (owner == (partner + shards_of // 2) % shards_of)
    return jnp.where(strong, factor * result, result)


def shard_levels(stream_key, shape, shards, least, high):
    def one(position, blocks):
        draws = jax.random.uniform(jax.random.fold_in(jax.random.fold_in(stream_key, 6), position), (blocks,), jnp.float32, least / len(shards), high / len(shards))
        return jnp.repeat(jnp.exp(draws), shape[position] // blocks).reshape((-1,) + (1,) * (len(shape) - position - 1))

    gain = one(*shards[0])
    for cut in shards[1:]:
        gain = gain * one(*cut)
    return gain


def scatter_about(own_key, shape, deviation, bound, cuts=(), kind=jnp.bfloat16):
    entries = deviation * jax.random.normal(own_key, shape, jnp.float32)
    if cuts:
        entries = entries * shard_levels(own_key, shape, cuts, -0.22, 0.18)
    return jnp.clip(entries, -bound, bound).astype(kind)


def gaussian_with(rng, extent, spread, most, shards, heavy, kind=jnp.bfloat16):
    result = spread * jax.random.normal(rng, extent, jnp.float32)
    if shards:
        result = result * shard_levels(rng, extent, shards, -0.22, 0.18)
    return jnp.clip(with_spikes(result, jax.random.fold_in(rng, 3), *heavy), -most, most).astype(kind)


def setup_inputs(seed: int = 0) -> dict:
    splits = jax.random.split(jax.random.key(seed), 11)
    file_lengths = draw_file_lengths(jax.random.fold_in(splits[10], 71), 0)
    queries = scatter_about(splits[1], (STRETCH_TOTAL * QC, KEY_VALUE_HEADS * Q_PER_KV * HEAD_SIZE), 1.0, 6.0, ((0, 64), (1, 4)))
    out_grad = scatter_about(splits[2], (STRETCH_TOTAL * QC, KEY_VALUE_HEADS * Q_PER_KV * HEAD_SIZE), 1.0, 6.0, ((0, 64), (1, 4)))
    mem_key = scatter_about(splits[3], (STRETCH_TOTAL * MEMORY_ROWS, KEY_VALUE_HEADS * HEAD_SIZE), 1.0, 6.0, ((0, 64), (1, 4)))
    memory_values = scatter_about(splits[4], (STRETCH_TOTAL * MEMORY_ROWS, KEY_VALUE_HEADS * HEAD_SIZE), 1.0, 6.0, ((0, 64), (1, 4)))
    enc_rows = gaussian_with(splits[5], (STRETCH_TOTAL * MEMORY_ROWS, D), 1.0, 16.0, ((0, 64),), (0, 1, 64, 4.0))
    key_down = scatter_about(splits[6], (D, LR), D ** -0.5, 0.09375)
    key_up = scatter_about(splits[7], (LR, KEY_VALUE_HEADS * HEAD_SIZE), LR ** -0.5, 0.5, ((1, 4),))
    value_down = scatter_about(splits[8], (D, LR), D ** -0.5, 0.09375)
    value_up = scatter_about(splits[9], (LR, KEY_VALUE_HEADS * HEAD_SIZE), LR ** -0.5, 0.5, ((1, 4),))
    return dict(file_lengths=file_lengths, queries=queries, out_grad=out_grad, mem_key=mem_key, memory_values=memory_values, enc_rows=enc_rows, key_down=key_down, key_up=key_up, value_down=value_down, value_up=value_up)


def stretch_grads(query, dout, keys, values, valid):
    scale = HEAD_SIZE ** -0.5
    qf = query.astype(jnp.float32)
    kf = keys.astype(jnp.float32)
    vf = values.astype(jnp.float32)
    df = dout.astype(jnp.float32)
    score = jnp.einsum('qgmd,kgd->gmqk', qf, kf) * scale
    mask = valid[None, None, None, :]
    expo = jnp.where(mask, jnp.exp(jnp.where(mask, score, 0.0)), 0.0)
    prob = expo / jnp.sum(expo, axis=-1, keepdims=True)
    prob_b = prob.astype(jnp.bfloat16).astype(jnp.float32)
    outp = jnp.einsum('gmqk,kgd->qgmd', prob_b, vf)
    delta = jnp.sum(df * outp, axis=-1)
    dprob = jnp.einsum('qgmd,kgd->gmqk', df, vf)
    dscore = (prob * (dprob - jnp.transpose(delta, (1, 2, 0))[..., None])).astype(jnp.bfloat16).astype(jnp.float32)
    dkey = jnp.einsum('gmqk,qgmd->kgd', dscore, qf) * scale
    dval = jnp.einsum('gmqk,qgmd->kgd', prob_b, df)
    return dkey, dval


def reference(file_lengths, queries, out_grad, mem_key, memory_values, enc_rows, key_down, key_up, value_down, value_up):
    key_value_width = KEY_VALUE_HEADS * HEAD_SIZE
    starts = jnp.cumsum(file_lengths).astype(jnp.int32) - file_lengths
    stretch_ids = jnp.arange(STRETCH_TOTAL, dtype=jnp.int32)
    first = jnp.max(jnp.where(starts[None, :] <= stretch_ids[:, None], starts[None, :], 0), axis=1)
    pos = stretch_ids - first
    qall = queries.reshape(STRETCH_TOTAL, QC, KEY_VALUE_HEADS, Q_PER_KV, HEAD_SIZE)
    dall = out_grad.reshape(STRETCH_TOTAL, QC, KEY_VALUE_HEADS, Q_PER_KV, HEAD_SIZE)
    kpad = jnp.concatenate([jnp.zeros(((MAX_STRETCHES - 1) * MEMORY_ROWS, key_value_width), jnp.bfloat16), mem_key], 0).reshape(STRETCH_TOTAL + MAX_STRETCHES - 1, MEMORY_ROWS, KEY_VALUE_HEADS, HEAD_SIZE)
    value_padded = jnp.concatenate([jnp.zeros(((MAX_STRETCHES - 1) * MEMORY_ROWS, key_value_width), jnp.bfloat16), memory_values], 0).reshape(STRETCH_TOTAL + MAX_STRETCHES - 1, MEMORY_ROWS, KEY_VALUE_HEADS, HEAD_SIZE)
    block_ids = jnp.arange(MAX_STRETCHES, dtype=jnp.int32)

    def one(column_index):
        kwin = lax.dynamic_slice_in_dim(kpad, column_index, MAX_STRETCHES, 0)[::-1].reshape(MAX_STRETCHES * MEMORY_ROWS, KEY_VALUE_HEADS, HEAD_SIZE)
        value_span_rows = lax.dynamic_slice_in_dim(value_padded, column_index, MAX_STRETCHES, 0)[::-1].reshape(MAX_STRETCHES * MEMORY_ROWS, KEY_VALUE_HEADS, HEAD_SIZE)
        valid = jnp.repeat(block_ids <= pos[column_index], MEMORY_ROWS)
        dkey, dval = stretch_grads(qall[column_index], dall[column_index], kwin, value_span_rows, valid)
        return dkey.reshape(MAX_STRETCHES, MEMORY_ROWS, key_value_width), dval.reshape(MAX_STRETCHES, MEMORY_ROWS, key_value_width)

    contrib_k, contrib_v = lax.map(one, stretch_ids)
    key_sum = jnp.zeros((STRETCH_TOTAL, MEMORY_ROWS, key_value_width), jnp.float32)
    val_sum = jnp.zeros((STRETCH_TOTAL, MEMORY_ROWS, key_value_width), jnp.float32)
    for j in range(MAX_STRETCHES):
        pad = jnp.zeros((j, MEMORY_ROWS, key_value_width), jnp.float32)
        key_sum = key_sum + jnp.concatenate([contrib_k[j:, j], pad], 0)
        val_sum = val_sum + jnp.concatenate([contrib_v[j:, j], pad], 0)
    key_grad = key_sum.reshape(STRETCH_TOTAL * MEMORY_ROWS, key_value_width).astype(jnp.bfloat16)
    value_grad = val_sum.reshape(STRETCH_TOTAL * MEMORY_ROWS, key_value_width).astype(jnp.bfloat16)
    u_key = jnp.dot(enc_rows, key_down, preferred_element_type=jnp.float32).astype(jnp.bfloat16)
    u_value = jnp.dot(enc_rows, value_down, preferred_element_type=jnp.float32).astype(jnp.bfloat16)
    h_key = jnp.dot(key_grad, key_up.T, preferred_element_type=jnp.float32).astype(jnp.bfloat16)
    h_value = jnp.dot(value_grad, value_up.T, preferred_element_type=jnp.float32).astype(jnp.bfloat16)
    grad_key_down = jnp.dot(enc_rows.T, h_key, preferred_element_type=jnp.float32)
    grad_value_down = jnp.dot(enc_rows.T, h_value, preferred_element_type=jnp.float32)
    grad_key_up = jnp.dot(u_key.T, key_grad, preferred_element_type=jnp.float32)
    grad_value_up = jnp.dot(u_value.T, value_grad, preferred_element_type=jnp.float32)
    return grad_key_down, grad_value_down, grad_key_up, grad_value_up
```

```python
import jax
import jax.numpy as jnp
from jax import lax
from jax.sharding import PartitionSpec as P

HEAD_SIZE = 128
Q_PER_KV = 4


def passed_along(array, axis, by):
    devices = lax.axis_size(axis)
    pairs = [(i, i + by) for i in range(devices) if 0 <= i + by < devices]
    return lax.ppermute(array, axis, pairs)


def stretch_grads(query, dout, keys, values, valid):
    scale = HEAD_SIZE ** (-0.5)
    score = jnp.einsum("qgmd,kgd->gmqk", query, keys, preferred_element_type=jnp.float32) * scale
    mask = valid[None, None, None, :]
    expo = jnp.where(mask, jnp.exp(jnp.where(mask, score, 0.0)), 0.0)
    prob = expo / jnp.sum(expo, axis=-1, keepdims=True)
    prob_b = prob.astype(jnp.bfloat16)
    outp = jnp.einsum("gmqk,kgd->qgmd", prob_b, values, preferred_element_type=jnp.float32)
    delta = jnp.sum(dout.astype(jnp.float32) * outp, axis=-1)
    dprob = jnp.einsum("qgmd,kgd->gmqk", dout, values, preferred_element_type=jnp.float32)
    dscore = (prob * (dprob - jnp.transpose(delta, (1, 2, 0))[..., None])).astype(jnp.bfloat16)
    dkey = jnp.einsum("gmqk,qgmd->kgd", dscore, query, preferred_element_type=jnp.float32) * scale
    dval = jnp.einsum("gmqk,qgmd->kgd", prob_b, dout, preferred_element_type=jnp.float32)
    return (dkey, dval)


def on_device(
    file_lengths,
    queries,
    out_grad,
    mem_key,
    memory_values,
    enc_rows,
    key_down,
    key_up,
    value_down,
    value_up,
):
    wide_count = lax.axis_size("wide")
    span = min(8, wide_count // 2)
    rows = mem_key.shape[0]
    cols = mem_key.shape[1]
    local_heads = cols // HEAD_SIZE
    stretch = lax.axis_index("wide")
    starts = jnp.cumsum(file_lengths) - file_lengths
    first = jnp.max(jnp.where(starts <= stretch, starts, 0))
    position = stretch - first
    paired = jnp.stack([mem_key, memory_values])
    blocks = [paired]
    for offset in range(1, span):
        blocks.append(passed_along(paired, "wide", offset))
    window = jnp.stack(blocks)
    keys = window[:, 0].reshape(span * rows, local_heads, HEAD_SIZE)
    values = window[:, 1].reshape(span * rows, local_heads, HEAD_SIZE)
    valid = jnp.repeat(jnp.arange(span, dtype=jnp.int32) <= position, rows)
    query = queries.reshape(queries.shape[0], local_heads, Q_PER_KV, HEAD_SIZE)
    dout = out_grad.reshape(out_grad.shape[0], local_heads, Q_PER_KV, HEAD_SIZE)
    dkey, dval = stretch_grads(query, dout, keys, values, valid)
    contrib = jnp.stack([dkey.reshape(span, rows, cols), dval.reshape(span, rows, cols)], 1)
    total = contrib[0]
    for offset in range(1, span):
        total = total + passed_along(contrib[offset], "wide", -offset)
    key_grad = total[0].astype(jnp.bfloat16)
    value_grad = total[1].astype(jnp.bfloat16)
    u_key = jnp.dot(enc_rows, key_down, preferred_element_type=jnp.float32).astype(jnp.bfloat16)
    u_value = jnp.dot(enc_rows, value_down, preferred_element_type=jnp.float32).astype(jnp.bfloat16)
    part_key = jnp.dot(key_grad, key_up.T, preferred_element_type=jnp.float32)
    part_value = jnp.dot(value_grad, value_up.T, preferred_element_type=jnp.float32)
    narrow_count = lax.axis_size("narrow")
    rank = part_key.shape[1]
    piece = rank // narrow_count
    parts = jnp.stack(
        [part_key.reshape(rows, narrow_count, piece), part_value.reshape(rows, narrow_count, piece)], 2
    )
    h_both = lax.psum_scatter(parts, "narrow", scatter_dimension=1, tiled=True)
    h_both = h_both.reshape(rows, 2 * piece).astype(jnp.bfloat16)
    up_key = jnp.dot(u_key.T, key_grad, preferred_element_type=jnp.float32)
    up_value = jnp.dot(u_value.T, value_grad, preferred_element_type=jnp.float32)
    down = jnp.dot(enc_rows.T, h_both, preferred_element_type=jnp.float32)
    down = lax.psum_scatter(down, "wide", scatter_dimension=0, tiled=True)
    up_key, up_value = lax.psum((up_key, up_value), "wide")
    share = down.shape[0]
    down = lax.all_gather(down.reshape(share, 2, piece), "narrow", axis=2, tiled=False)
    down = down.reshape(share, 2, rank)
    down_key = down[:, 0]
    down_value = down[:, 1]
    return (down_key, down_value, up_key, up_value)


def solution(mesh):
    placed = (
        P(),
        P("wide", "narrow"),
        P("wide", "narrow"),
        P("wide", "narrow"),
        P("wide", "narrow"),
        P("wide", None),
        P(),
        P(None, "narrow"),
        P(),
        P(None, "narrow"),
    )
    return jax.shard_map(
        on_device,
        mesh=mesh,
        in_specs=placed,
        out_specs=(P("wide", None), P("wide", None), P(None, "narrow"), P(None, "narrow")),
        check_vma=False,
    )
```

```python
import jax
import jax.numpy as jnp
from jax import lax
from jax.sharding import PartitionSpec as P

HEAD_SIZE = 128
Q_PER_KV = 4


def passed_along(array, axis, by):
    devices = lax.axis_size(axis)
    pairs = [(i, i + by) for i in range(devices) if 0 <= i + by < devices]
    return lax.ppermute(array, axis, pairs)


def swapped(array, axis, bit):
    devices = lax.axis_size(axis)
    pairs = [(i, i ^ bit) for i in range(devices)]
    return lax.ppermute(array, axis, pairs)


def scattered_sum(x, axis):
    devices = lax.axis_size(axis)
    me = lax.axis_index(axis)
    bit = 1
    while bit < devices:
        pair = x.reshape(x.shape[0] // 2, 2, *x.shape[1:])
        mine = (me // bit) % 2
        keep = lax.dynamic_index_in_dim(pair, mine, axis=1, keepdims=False)
        give = lax.dynamic_index_in_dim(pair, 1 - mine, axis=1, keepdims=False)
        x = keep + swapped(give, axis, bit)
        bit *= 2
    return x[0]


def gathered(y, axis):
    devices = lax.axis_size(axis)
    me = lax.axis_index(axis)
    y = y[None]
    bit = devices // 2
    while bit >= 1:
        other = swapped(y, axis, bit)
        first = (me // bit) % 2 == 0
        low = jnp.where(first, y, other)
        high = jnp.where(first, other, y)
        y = jnp.stack([low, high], 1).reshape(y.shape[0] * 2, *y.shape[1:])
        bit //= 2
    return y


def stretch_grads(query, dout, keys, values, valid):
    scale = HEAD_SIZE ** (-0.5)
    score = jnp.einsum("qgmd,kgd->gmqk", query, keys, preferred_element_type=jnp.float32) * scale
    mask = valid[None, None, None, :]
    expo = jnp.where(mask, jnp.exp(jnp.where(mask, score, 0.0)), 0.0)
    prob = expo / jnp.sum(expo, axis=-1, keepdims=True)
    prob_b = prob.astype(jnp.bfloat16)
    outp = jnp.einsum("gmqk,kgd->qgmd", prob_b, values, preferred_element_type=jnp.float32)
    delta = jnp.sum(dout.astype(jnp.float32) * outp, axis=-1)
    dprob = jnp.einsum("qgmd,kgd->gmqk", dout, values, preferred_element_type=jnp.float32)
    dscore = (prob * (dprob - jnp.transpose(delta, (1, 2, 0))[..., None])).astype(jnp.bfloat16)
    dkey = jnp.einsum("gmqk,qgmd->kgd", dscore, query, preferred_element_type=jnp.float32) * scale
    dval = jnp.einsum("gmqk,qgmd->kgd", prob_b, dout, preferred_element_type=jnp.float32)
    return (dkey, dval)


def on_device(
    file_lengths,
    queries,
    out_grad,
    mem_key,
    memory_values,
    enc_rows,
    key_down,
    key_up,
    value_down,
    value_up,
):
    wide_count = lax.axis_size("wide")
    narrow_count = lax.axis_size("narrow")
    span = 8
    rows = mem_key.shape[0]
    cols = mem_key.shape[1]
    local_heads = cols // HEAD_SIZE
    stretch = lax.axis_index("wide")
    starts = jnp.cumsum(file_lengths) - file_lengths
    first = jnp.max(jnp.where(starts <= stretch, starts, 0))
    position = stretch - first
    window = jnp.stack([mem_key, memory_values])[None]
    reach = 1
    while reach < span:
        window = jnp.concatenate([window, passed_along(window, "wide", reach)], 0)
        reach *= 2
    keys = window[:, 0].reshape(span * rows, local_heads, HEAD_SIZE)
    values = window[:, 1].reshape(span * rows, local_heads, HEAD_SIZE)
    valid = jnp.repeat(jnp.arange(span, dtype=jnp.int32) <= position, rows)
    query = queries.reshape(queries.shape[0], local_heads, Q_PER_KV, HEAD_SIZE)
    dout = out_grad.reshape(out_grad.shape[0], local_heads, Q_PER_KV, HEAD_SIZE)
    dkey, dval = stretch_grads(query, dout, keys, values, valid)
    contrib = jnp.stack([dkey.reshape(span, rows, cols), dval.reshape(span, rows, cols)], 1)
    reach = span // 2
    while reach >= 1:
        contrib = contrib[:reach] + passed_along(contrib[reach : 2 * reach], "wide", -reach)
        reach //= 2
    total = contrib[0]
    key_grad = total[0].astype(jnp.bfloat16)
    value_grad = total[1].astype(jnp.bfloat16)
    u_key = jnp.dot(enc_rows, key_down, preferred_element_type=jnp.float32).astype(jnp.bfloat16)
    u_value = jnp.dot(enc_rows, value_down, preferred_element_type=jnp.float32).astype(jnp.bfloat16)
    part_key = jnp.dot(key_grad, key_up.T, preferred_element_type=jnp.float32)
    part_value = jnp.dot(value_grad, value_up.T, preferred_element_type=jnp.float32)
    rank = part_key.shape[1]
    piece = rank // narrow_count
    parts = jnp.concatenate(
        [
            part_key.reshape(rows, narrow_count, piece).transpose(1, 0, 2),
            part_value.reshape(rows, narrow_count, piece).transpose(1, 0, 2),
        ],
        2,
    )
    h_both = scattered_sum(parts, "narrow").astype(jnp.bfloat16)
    up_key = jnp.dot(u_key.T, key_grad, preferred_element_type=jnp.float32)
    up_value = jnp.dot(u_value.T, value_grad, preferred_element_type=jnp.float32)
    down = jnp.dot(enc_rows.T, h_both, preferred_element_type=jnp.float32)
    width = down.shape[0] // wide_count
    up_both = jnp.stack([up_key, up_value]).reshape(wide_count, -1)
    joined = jnp.concatenate([down.reshape(wide_count, width * 2 * piece), up_both], 1)
    joined = scattered_sum(joined, "wide")
    down = joined[: width * 2 * piece].reshape(width, 2, piece)
    up_both = gathered(joined[width * 2 * piece :], "wide").reshape(2, rank, cols)
    down = gathered(down, "narrow").transpose(1, 2, 0, 3).reshape(width, 2, rank)
    return (down[:, 0], down[:, 1], up_both[0], up_both[1])


def solution(mesh):
    placed = (
        P(),
        P("wide", "narrow"),
        P("wide", "narrow"),
        P("wide", "narrow"),
        P("wide", "narrow"),
        P("wide", None),
        P(),
        P(None, "narrow"),
        P(),
        P(None, "narrow"),
    )
    return jax.shard_map(
        on_device,
        mesh=mesh,
        in_specs=placed,
        out_specs=(P("wide", None), P("wide", None), P(None, "narrow"), P(None, "narrow")),
        check_vma=False,
    )
```

```python
import jax
import jax.numpy as jnp
from jax import lax
from jax.sharding import PartitionSpec as P

HEAD_SIZE = 128
Q_PER_KV = 4


def passed_along(array, axis, by):
    devices = lax.axis_size(axis)
    pairs = [(i, i + by) for i in range(devices) if 0 <= i + by < devices]
    return lax.ppermute(array, axis, pairs)


def swapped(array, axis, bit):
    devices = lax.axis_size(axis)
    pairs = [(i, i ^ bit) for i in range(devices)]
    return lax.ppermute(array, axis, pairs)


def scattered_sum(x, axis):
    devices = lax.axis_size(axis)
    me = lax.axis_index(axis)
    bit = 1
    while bit < devices:
        pair = x.reshape(x.shape[0] // 2, 2, *x.shape[1:])
        mine = (me // bit) % 2
        keep = lax.dynamic_index_in_dim(pair, mine, axis=1, keepdims=False)
        give = lax.dynamic_index_in_dim(pair, 1 - mine, axis=1, keepdims=False)
        x = keep + swapped(give, axis, bit)
        bit *= 2
    return x[0]


def scattered_sum_with(x, whole, axis):
    devices = lax.axis_size(axis)
    me = lax.axis_index(axis)
    bit = 1
    while bit < devices:
        pair = x.reshape(x.shape[0] // 2, 2, *x.shape[1:])
        mine = (me // bit) % 2
        keep = lax.dynamic_index_in_dim(pair, mine, axis=1, keepdims=False)
        give = lax.dynamic_index_in_dim(pair, 1 - mine, axis=1, keepdims=False)
        message = jnp.concatenate([give.reshape(-1), whole.reshape(-1)])
        back = swapped(message, axis, bit)
        x = keep + back[: give.size].reshape(give.shape)
        whole = whole + back[give.size :].reshape(whole.shape)
        bit *= 2
    return x[0], whole


def gathered(y, axis):
    devices = lax.axis_size(axis)
    me = lax.axis_index(axis)
    y = y[None]
    bit = devices // 2
    while bit >= 1:
        other = swapped(y, axis, bit)
        first = (me // bit) % 2 == 0
        low = jnp.where(first, y, other)
        high = jnp.where(first, other, y)
        y = jnp.stack([low, high], 1).reshape(y.shape[0] * 2, *y.shape[1:])
        bit //= 2
    return y


def stretch_grads(query, dout, keys, values, valid):
    scale = HEAD_SIZE ** (-0.5)
    score = jnp.einsum("qgmd,kgd->gmqk", query, keys, preferred_element_type=jnp.float32) * scale
    mask = valid[None, None, None, :]
    expo = jnp.where(mask, jnp.exp(jnp.where(mask, score, 0.0)), 0.0)
    prob = expo / jnp.sum(expo, axis=-1, keepdims=True)
    prob_b = prob.astype(jnp.bfloat16)
    outp = jnp.einsum("gmqk,kgd->qgmd", prob_b, values, preferred_element_type=jnp.float32)
    delta = jnp.sum(dout.astype(jnp.float32) * outp, axis=-1)
    dprob = jnp.einsum("qgmd,kgd->gmqk", dout, values, preferred_element_type=jnp.float32)
    dscore = (prob * (dprob - jnp.transpose(delta, (1, 2, 0))[..., None])).astype(jnp.bfloat16)
    dkey = jnp.einsum("gmqk,qgmd->kgd", dscore, query, preferred_element_type=jnp.float32) * scale
    dval = jnp.einsum("gmqk,qgmd->kgd", prob_b, dout, preferred_element_type=jnp.float32)
    return (dkey, dval)


def on_device(
    file_lengths,
    queries,
    out_grad,
    mem_key,
    memory_values,
    enc_rows,
    key_down,
    key_up,
    value_down,
    value_up,
):
    wide_count = lax.axis_size("wide")
    narrow_count = lax.axis_size("narrow")
    span = 8
    rows = mem_key.shape[0]
    cols = mem_key.shape[1]
    local_heads = cols // HEAD_SIZE
    stretch = lax.axis_index("wide")
    starts = jnp.cumsum(file_lengths) - file_lengths
    first = jnp.max(jnp.where(starts <= stretch, starts, 0))
    position = stretch - first
    window = jnp.stack([mem_key, memory_values])[None]
    reach = 1
    while reach < span:
        window = jnp.concatenate([window, passed_along(window, "wide", reach)], 0)
        reach *= 2
    keys = window[:, 0].reshape(span * rows, local_heads, HEAD_SIZE)
    values = window[:, 1].reshape(span * rows, local_heads, HEAD_SIZE)
    valid = jnp.repeat(jnp.arange(span, dtype=jnp.int32) <= position, rows)
    query = queries.reshape(queries.shape[0], local_heads, Q_PER_KV, HEAD_SIZE)
    dout = out_grad.reshape(out_grad.shape[0], local_heads, Q_PER_KV, HEAD_SIZE)
    dkey, dval = stretch_grads(query, dout, keys, values, valid)
    contrib = jnp.stack([dkey.reshape(span, rows, cols), dval.reshape(span, rows, cols)], 1)
    reach = span // 2
    while reach >= 1:
        contrib = contrib[:reach] + passed_along(contrib[reach : 2 * reach], "wide", -reach)
        reach //= 2
    total = contrib[0]
    key_grad = total[0].astype(jnp.bfloat16)
    value_grad = total[1].astype(jnp.bfloat16)
    u_key = jnp.dot(enc_rows, key_down, preferred_element_type=jnp.float32).astype(jnp.bfloat16)
    u_value = jnp.dot(enc_rows, value_down, preferred_element_type=jnp.float32).astype(jnp.bfloat16)
    part_key = jnp.dot(key_grad, key_up.T, preferred_element_type=jnp.float32)
    part_value = jnp.dot(value_grad, value_up.T, preferred_element_type=jnp.float32)
    rank = part_key.shape[1]
    piece = rank // narrow_count
    parts = jnp.concatenate(
        [
            part_key.reshape(rows, narrow_count, piece).transpose(1, 0, 2),
            part_value.reshape(rows, narrow_count, piece).transpose(1, 0, 2),
        ],
        2,
    )
    h_both = scattered_sum(parts, "narrow").astype(jnp.bfloat16)
    up_key = jnp.dot(u_key.T, key_grad, preferred_element_type=jnp.float32)
    up_value = jnp.dot(u_value.T, value_grad, preferred_element_type=jnp.float32)
    down = jnp.dot(enc_rows.T, h_both, preferred_element_type=jnp.float32)
    width = down.shape[0] // wide_count
    down, up_both = scattered_sum_with(down.reshape(wide_count, width * 2 * piece), jnp.stack([up_key, up_value]), "wide")
    down = down.reshape(width, 2, piece)
    down = gathered(down, "narrow").transpose(1, 2, 0, 3).reshape(width, 2, rank)
    return (down[:, 0], down[:, 1], up_both[0], up_both[1])


def solution(mesh):
    placed = (
        P(),
        P("wide", "narrow"),
        P("wide", "narrow"),
        P("wide", "narrow"),
        P("wide", "narrow"),
        P("wide", None),
        P(),
        P(None, "narrow"),
        P(),
        P(None, "narrow"),
    )
    return jax.shard_map(
        on_device,
        mesh=mesh,
        in_specs=placed,
        out_specs=(P("wide", None), P("wide", None), P(None, "narrow"), P(None, "narrow")),
        check_vma=False,
    )
```

```python
import jax
import jax.numpy as jnp
from jax import lax
from jax.experimental import pallas as pl
from jax.experimental.pallas import tpu as pltpu
from jax.sharding import PartitionSpec as P

HEAD_SIZE = 128
Q_PER_KV = 4


def passed_along(array, axis, by):
    devices = lax.axis_size(axis)
    pairs = [(i, i + by) for i in range(devices) if 0 <= i + by < devices]
    return lax.ppermute(array, axis, pairs)


def swapped(array, axis, bit):
    devices = lax.axis_size(axis)
    pairs = [(i, i ^ bit) for i in range(devices)]
    return lax.ppermute(array, axis, pairs)


def scattered_sum(x, axis):
    devices = lax.axis_size(axis)
    me = lax.axis_index(axis)
    bit = 1
    while bit < devices:
        pair = x.reshape(x.shape[0] // 2, 2, *x.shape[1:])
        mine = (me // bit) % 2
        keep = lax.dynamic_index_in_dim(pair, mine, axis=1, keepdims=False)
        give = lax.dynamic_index_in_dim(pair, 1 - mine, axis=1, keepdims=False)
        x = keep + swapped(give, axis, bit)
        bit *= 2
    return x[0]


def gathered(y, axis):
    devices = lax.axis_size(axis)
    me = lax.axis_index(axis)
    y = y[None]
    bit = devices // 2
    while bit >= 1:
        other = swapped(y, axis, bit)
        first = (me // bit) % 2 == 0
        low = jnp.where(first, y, other)
        high = jnp.where(first, other, y)
        y = jnp.stack([low, high], 1).reshape(y.shape[0] * 2, *y.shape[1:])
        bit //= 2
    return y


def attention_body(pos_ref, q_ref, do_ref, k_ref, v_ref, dk_ref, dv_ref):
    m = pl.program_id(1)
    scale = HEAD_SIZE ** (-0.5)
    q = q_ref[...]
    do = do_ref[...]
    k = k_ref[...]
    v = v_ref[...]
    s = lax.dot_general(q, k, (((1,), (1,)), ((), ())), preferred_element_type=jnp.float32) * scale
    block = lax.broadcasted_iota(jnp.int32, s.shape, 1) // 128
    mask = block <= pos_ref[0]
    expo = jnp.where(mask, jnp.exp(jnp.where(mask, s, 0.0)), 0.0)
    prob = expo / jnp.sum(expo, axis=-1, keepdims=True)
    prob_b = prob.astype(jnp.bfloat16)
    outp = jnp.dot(prob_b, v, preferred_element_type=jnp.float32)
    delta = jnp.sum(do.astype(jnp.float32) * outp, axis=-1, keepdims=True)
    dprob = lax.dot_general(do, v, (((1,), (1,)), ((), ())), preferred_element_type=jnp.float32)
    dscore = (prob * (dprob - delta)).astype(jnp.bfloat16)
    dk = lax.dot_general(dscore, q, (((0,), (0,)), ((), ())), preferred_element_type=jnp.float32)
    dv = lax.dot_general(prob_b, do, (((0,), (0,)), ((), ())), preferred_element_type=jnp.float32)

    @pl.when(m == 0)
    def _():
        dk_ref[...] = dk
        dv_ref[...] = dv

    @pl.when(m > 0)
    def _():
        dk_ref[...] += dk
        dv_ref[...] += dv


def attention_grads(position, queries, out_grad, keys, values):
    tokens = queries.shape[0]
    window_rows, cols = keys.shape
    heads = cols // HEAD_SIZE
    scale = HEAD_SIZE ** (-0.5)
    grid_spec = pltpu.PrefetchScalarGridSpec(
        num_scalar_prefetch=1,
        grid=(heads, Q_PER_KV),
        in_specs=[
            pl.BlockSpec((tokens, HEAD_SIZE), lambda g, m, p: (0, g * Q_PER_KV + m)),
            pl.BlockSpec((tokens, HEAD_SIZE), lambda g, m, p: (0, g * Q_PER_KV + m)),
            pl.BlockSpec((window_rows, HEAD_SIZE), lambda g, m, p: (0, g)),
            pl.BlockSpec((window_rows, HEAD_SIZE), lambda g, m, p: (0, g)),
        ],
        out_specs=[
            pl.BlockSpec((window_rows, HEAD_SIZE), lambda g, m, p: (0, g)),
            pl.BlockSpec((window_rows, HEAD_SIZE), lambda g, m, p: (0, g)),
        ],
    )
    dk, dv = pl.pallas_call(
        attention_body,
        grid_spec=grid_spec,
        out_shape=[jax.ShapeDtypeStruct((window_rows, cols), jnp.float32)] * 2,
        compiler_params=pltpu.CompilerParams(dimension_semantics=("arbitrary", "arbitrary")),
    )(position.reshape(1).astype(jnp.int32), queries, out_grad, keys, values)
    return dk * scale, dv


def on_device(
    file_lengths,
    queries,
    out_grad,
    mem_key,
    memory_values,
    enc_rows,
    key_down,
    key_up,
    value_down,
    value_up,
):
    wide_count = lax.axis_size("wide")
    narrow_count = lax.axis_size("narrow")
    span = 8
    rows = mem_key.shape[0]
    cols = mem_key.shape[1]
    local_heads = cols // HEAD_SIZE
    stretch = lax.axis_index("wide")
    starts = jnp.cumsum(file_lengths) - file_lengths
    first = jnp.max(jnp.where(starts <= stretch, starts, 0))
    position = stretch - first
    window = jnp.stack([mem_key, memory_values])[None]
    reach = 1
    while reach < span:
        window = jnp.concatenate([window, passed_along(window, "wide", reach)], 0)
        reach *= 2
    keys = window[:, 0].reshape(span * rows, cols)
    values = window[:, 1].reshape(span * rows, cols)
    dkey, dval = attention_grads(position, queries, out_grad, keys, values)
    contrib = jnp.stack([dkey.reshape(span, rows, cols), dval.reshape(span, rows, cols)], 1)
    reach = span // 2
    while reach >= 1:
        contrib = contrib[:reach] + passed_along(contrib[reach : 2 * reach], "wide", -reach)
        reach //= 2
    total = contrib[0]
    key_grad = total[0].astype(jnp.bfloat16)
    value_grad = total[1].astype(jnp.bfloat16)
    u_key = jnp.dot(enc_rows, key_down, preferred_element_type=jnp.float32).astype(jnp.bfloat16)
    u_value = jnp.dot(enc_rows, value_down, preferred_element_type=jnp.float32).astype(jnp.bfloat16)
    part_key = jnp.dot(key_grad, key_up.T, preferred_element_type=jnp.float32)
    part_value = jnp.dot(value_grad, value_up.T, preferred_element_type=jnp.float32)
    rank = part_key.shape[1]
    piece = rank // narrow_count
    parts = jnp.concatenate(
        [
            part_key.reshape(rows, narrow_count, piece).transpose(1, 0, 2),
            part_value.reshape(rows, narrow_count, piece).transpose(1, 0, 2),
        ],
        2,
    )
    h_both = scattered_sum(parts, "narrow").astype(jnp.bfloat16)
    up_key = jnp.dot(u_key.T, key_grad, preferred_element_type=jnp.float32)
    up_value = jnp.dot(u_value.T, value_grad, preferred_element_type=jnp.float32)
    down = jnp.dot(enc_rows.T, h_both, preferred_element_type=jnp.float32)
    width = down.shape[0] // wide_count
    up_both = jnp.stack([up_key, up_value]).reshape(wide_count, -1)
    joined = jnp.concatenate([down.reshape(wide_count, width * 2 * piece), up_both], 1)
    joined = scattered_sum(joined, "wide")
    down = joined[: width * 2 * piece].reshape(width, 2, piece)
    up_both = gathered(joined[width * 2 * piece :], "wide").reshape(2, rank, cols)
    down = gathered(down, "narrow").transpose(1, 2, 0, 3).reshape(width, 2, rank)
    return (down[:, 0], down[:, 1], up_both[0], up_both[1])


def solution(mesh):
    placed = (
        P(),
        P("wide", "narrow"),
        P("wide", "narrow"),
        P("wide", "narrow"),
        P("wide", "narrow"),
        P("wide", None),
        P(),
        P(None, "narrow"),
        P(),
        P(None, "narrow"),
    )
    return jax.shard_map(
        on_device,
        mesh=mesh,
        in_specs=placed,
        out_specs=(P("wide", None), P("wide", None), P(None, "narrow"), P(None, "narrow")),
        check_vma=False,
    )
```

```python
import jax
import jax.numpy as jnp
from jax import lax
from jax.experimental import pallas as pl
from jax.experimental.pallas import tpu as pltpu
from jax.sharding import PartitionSpec as P

HEAD_SIZE = 128
Q_PER_KV = 4


def passed_along(array, axis, by):
    devices = lax.axis_size(axis)
    pairs = [(i, i + by) for i in range(devices) if 0 <= i + by < devices]
    return lax.ppermute(array, axis, pairs)


def digit_steps(devices):
    steps = []
    low = 1
    while low < devices:
        radix = 4 if devices % (low * 4) == 0 else 2
        steps.append((low, radix))
        low *= radix
    return steps


def xor_partner(array, axis, mask):
    devices = lax.axis_size(axis)
    return lax.ppermute(array, axis, [(i, i ^ mask) for i in range(devices)])


def scattered_sum(x, axis):
    me = lax.axis_index(axis)
    for low, radix in digit_steps(lax.axis_size(axis)):
        group = x.reshape(x.shape[0] // radix, radix, *x.shape[1:])
        mine = (me // low) % radix
        x = lax.dynamic_index_in_dim(group, mine, axis=1, keepdims=False)
        for t in range(1, radix):
            give = lax.dynamic_index_in_dim(group, jnp.bitwise_xor(mine, t), axis=1, keepdims=False)
            x = x + xor_partner(give, axis, t * low)
    return x[0]


def gathered(y, axis):
    me = lax.axis_index(axis)
    y = y[None]
    for low, radix in reversed(digit_steps(lax.axis_size(axis))):
        mine = (me // low) % radix
        got = [y] + [xor_partner(y, axis, t * low) for t in range(1, radix)]
        order = jnp.bitwise_xor(jnp.arange(radix, dtype=mine.dtype), mine)
        y = jnp.take(jnp.stack(got, 1), order, axis=1)
        y = y.reshape(y.shape[0] * radix, *y.shape[2:])
    return y


def attention_body(pos_ref, q_ref, do_ref, k_ref, v_ref, dk_ref, dv_ref):
    m = pl.program_id(1)
    scale = HEAD_SIZE ** (-0.5)
    q = q_ref[...]
    do = do_ref[...]
    k = k_ref[...]
    v = v_ref[...]
    s = lax.dot_general(q, k, (((1,), (1,)), ((), ())), preferred_element_type=jnp.float32) * scale
    block = lax.broadcasted_iota(jnp.int32, s.shape, 1) // 128
    mask = block <= pos_ref[0]
    expo = jnp.where(mask, jnp.exp(jnp.where(mask, s, 0.0)), 0.0)
    prob = expo / jnp.sum(expo, axis=-1, keepdims=True)
    prob_b = prob.astype(jnp.bfloat16)
    outp = jnp.dot(prob_b, v, preferred_element_type=jnp.float32)
    delta = jnp.sum(do.astype(jnp.float32) * outp, axis=-1, keepdims=True)
    dprob = lax.dot_general(do, v, (((1,), (1,)), ((), ())), preferred_element_type=jnp.float32)
    dscore = (prob * (dprob - delta)).astype(jnp.bfloat16)
    dk = lax.dot_general(dscore, q, (((0,), (0,)), ((), ())), preferred_element_type=jnp.float32)
    dv = lax.dot_general(prob_b, do, (((0,), (0,)), ((), ())), preferred_element_type=jnp.float32)

    @pl.when(m == 0)
    def _():
        dk_ref[...] = dk
        dv_ref[...] = dv

    @pl.when(m > 0)
    def _():
        dk_ref[...] += dk
        dv_ref[...] += dv


def attention_grads(position, queries, out_grad, keys, values):
    tokens = queries.shape[0]
    window_rows, cols = keys.shape
    heads = cols // HEAD_SIZE
    scale = HEAD_SIZE ** (-0.5)
    grid_spec = pltpu.PrefetchScalarGridSpec(
        num_scalar_prefetch=1,
        grid=(heads, Q_PER_KV),
        in_specs=[
            pl.BlockSpec((tokens, HEAD_SIZE), lambda g, m, p: (0, g * Q_PER_KV + m)),
            pl.BlockSpec((tokens, HEAD_SIZE), lambda g, m, p: (0, g * Q_PER_KV + m)),
            pl.BlockSpec((window_rows, HEAD_SIZE), lambda g, m, p: (0, g)),
            pl.BlockSpec((window_rows, HEAD_SIZE), lambda g, m, p: (0, g)),
        ],
        out_specs=[
            pl.BlockSpec((window_rows, HEAD_SIZE), lambda g, m, p: (0, g)),
            pl.BlockSpec((window_rows, HEAD_SIZE), lambda g, m, p: (0, g)),
        ],
    )
    dk, dv = pl.pallas_call(
        attention_body,
        grid_spec=grid_spec,
        out_shape=[jax.ShapeDtypeStruct((window_rows, cols), jnp.float32)] * 2,
        compiler_params=pltpu.CompilerParams(dimension_semantics=("arbitrary", "arbitrary")),
    )(position.reshape(1).astype(jnp.int32), queries, out_grad, keys, values)
    return dk * scale, dv


def on_device(
    file_lengths,
    queries,
    out_grad,
    mem_key,
    memory_values,
    enc_rows,
    key_down,
    key_up,
    value_down,
    value_up,
):
    wide_count = lax.axis_size("wide")
    narrow_count = lax.axis_size("narrow")
    span = 8
    rows = mem_key.shape[0]
    cols = mem_key.shape[1]
    local_heads = cols // HEAD_SIZE
    stretch = lax.axis_index("wide")
    starts = jnp.cumsum(file_lengths) - file_lengths
    first = jnp.max(jnp.where(starts <= stretch, starts, 0))
    position = stretch - first
    window = jnp.stack([mem_key, memory_values])[None]
    reach = 1
    while reach < span:
        window = jnp.concatenate([window, passed_along(window, "wide", reach)], 0)
        reach *= 2
    keys = window[:, 0].reshape(span * rows, cols)
    values = window[:, 1].reshape(span * rows, cols)
    dkey, dval = attention_grads(position, queries, out_grad, keys, values)
    contrib = jnp.stack([dkey.reshape(span, rows, cols), dval.reshape(span, rows, cols)], 1)
    reach = span // 2
    while reach >= 1:
        contrib = contrib[:reach] + passed_along(contrib[reach : 2 * reach], "wide", -reach)
        reach //= 2
    total = contrib[0]
    key_grad = total[0].astype(jnp.bfloat16)
    value_grad = total[1].astype(jnp.bfloat16)
    u_key = jnp.dot(enc_rows, key_down, preferred_element_type=jnp.float32).astype(jnp.bfloat16)
    u_value = jnp.dot(enc_rows, value_down, preferred_element_type=jnp.float32).astype(jnp.bfloat16)
    part_key = jnp.dot(key_grad, key_up.T, preferred_element_type=jnp.float32)
    part_value = jnp.dot(value_grad, value_up.T, preferred_element_type=jnp.float32)
    rank = part_key.shape[1]
    piece = rank // narrow_count
    parts = jnp.concatenate(
        [
            part_key.reshape(rows, narrow_count, piece).transpose(1, 0, 2),
            part_value.reshape(rows, narrow_count, piece).transpose(1, 0, 2),
        ],
        2,
    )
    h_both = scattered_sum(parts, "narrow").astype(jnp.bfloat16)
    up_key = jnp.dot(u_key.T, key_grad, preferred_element_type=jnp.float32)
    up_value = jnp.dot(u_value.T, value_grad, preferred_element_type=jnp.float32)
    down = jnp.dot(enc_rows.T, h_both, preferred_element_type=jnp.float32)
    width = down.shape[0] // wide_count
    up_both = jnp.stack([up_key, up_value]).reshape(wide_count, -1)
    joined = jnp.concatenate([down.reshape(wide_count, width * 2 * piece), up_both], 1)
    joined = scattered_sum(joined, "wide")
    down = joined[: width * 2 * piece].reshape(width, 2, piece)
    up_both = gathered(joined[width * 2 * piece :], "wide").reshape(2, rank, cols)
    down = gathered(down, "narrow").transpose(1, 2, 0, 3).reshape(width, 2, rank)
    return (down[:, 0], down[:, 1], up_both[0], up_both[1])


def solution(mesh):
    placed = (
        P(),
        P("wide", "narrow"),
        P("wide", "narrow"),
        P("wide", "narrow"),
        P("wide", "narrow"),
        P("wide", None),
        P(),
        P(None, "narrow"),
        P(),
        P(None, "narrow"),
    )
    return jax.shard_map(
        on_device,
        mesh=mesh,
        in_specs=placed,
        out_specs=(P("wide", None), P("wide", None), P(None, "narrow"), P(None, "narrow")),
        check_vma=False,
    )
```

```python
import jax
import jax.numpy as jnp
from jax import lax
from jax.experimental import pallas as pl
from jax.experimental.pallas import tpu as pltpu
from jax.sharding import PartitionSpec as P

HEAD_SIZE = 128
Q_PER_KV = 4


def passed_along(array, axis, by):
    devices = lax.axis_size(axis)
    pairs = [(i, i + by) for i in range(devices) if 0 <= i + by < devices]
    return lax.ppermute(array, axis, pairs)


def digit_steps(devices):
    steps = []
    low = 1
    while low < devices:
        radix = 4 if devices % (low * 4) == 0 else 2
        steps.append((low, radix))
        low *= radix
    return steps


def xor_partner(array, axis, mask):
    devices = lax.axis_size(axis)
    return lax.ppermute(array, axis, [(i, i ^ mask) for i in range(devices)])


def scattered_sum(x, axis):
    me = lax.axis_index(axis)
    for low, radix in digit_steps(lax.axis_size(axis)):
        group = x.reshape(x.shape[0] // radix, radix, *x.shape[1:])
        mine = (me // low) % radix
        x = lax.dynamic_index_in_dim(group, mine, axis=1, keepdims=False)
        for t in range(1, radix):
            give = lax.dynamic_index_in_dim(group, jnp.bitwise_xor(mine, t), axis=1, keepdims=False)
            x = x + xor_partner(give, axis, t * low)
    return x[0]


def gathered(y, axis):
    me = lax.axis_index(axis)
    y = y[None]
    for low, radix in reversed(digit_steps(lax.axis_size(axis))):
        mine = (me // low) % radix
        got = [y] + [xor_partner(y, axis, t * low) for t in range(1, radix)]
        order = jnp.bitwise_xor(jnp.arange(radix, dtype=mine.dtype), mine)
        y = jnp.take(jnp.stack(got, 1), order, axis=1)
        y = y.reshape(y.shape[0] * radix, *y.shape[2:])
    return y


def attention_body(pos_ref, q_ref, do_ref, k_ref, v_ref, dk_ref, dv_ref):
    m = pl.program_id(1)
    scale = HEAD_SIZE ** (-0.5)
    q = q_ref[...]
    do = do_ref[...]
    k = k_ref[...]
    v = v_ref[...]
    s = lax.dot_general(q, k, (((1,), (1,)), ((), ())), preferred_element_type=jnp.float32) * scale
    block = lax.broadcasted_iota(jnp.int32, s.shape, 1) // 128
    mask = block <= pos_ref[0]
    expo = jnp.where(mask, jnp.exp(jnp.where(mask, s, 0.0)), 0.0)
    prob = expo / jnp.sum(expo, axis=-1, keepdims=True)
    prob_b = prob.astype(jnp.bfloat16)
    outp = jnp.dot(prob_b, v, preferred_element_type=jnp.float32)
    delta = jnp.sum(do.astype(jnp.float32) * outp, axis=-1, keepdims=True)
    dprob = lax.dot_general(do, v, (((1,), (1,)), ((), ())), preferred_element_type=jnp.float32)
    dscore = (prob * (dprob - delta)).astype(jnp.bfloat16)
    dk = lax.dot_general(dscore, q, (((0,), (0,)), ((), ())), preferred_element_type=jnp.float32)
    dv = lax.dot_general(prob_b, do, (((0,), (0,)), ((), ())), preferred_element_type=jnp.float32)

    @pl.when(m == 0)
    def _():
        dk_ref[...] = dk
        dv_ref[...] = dv

    @pl.when(m > 0)
    def _():
        dk_ref[...] += dk
        dv_ref[...] += dv


def attention_grads(position, queries, out_grad, keys, values):
    tokens = queries.shape[0]
    window_rows, cols = keys.shape
    heads = cols // HEAD_SIZE
    scale = HEAD_SIZE ** (-0.5)
    grid_spec = pltpu.PrefetchScalarGridSpec(
        num_scalar_prefetch=1,
        grid=(heads, Q_PER_KV),
        in_specs=[
            pl.BlockSpec((tokens, HEAD_SIZE), lambda g, m, p: (0, g * Q_PER_KV + m)),
            pl.BlockSpec((tokens, HEAD_SIZE), lambda g, m, p: (0, g * Q_PER_KV + m)),
            pl.BlockSpec((window_rows, HEAD_SIZE), lambda g, m, p: (0, g)),
            pl.BlockSpec((window_rows, HEAD_SIZE), lambda g, m, p: (0, g)),
        ],
        out_specs=[
            pl.BlockSpec((window_rows, HEAD_SIZE), lambda g, m, p: (0, g)),
            pl.BlockSpec((window_rows, HEAD_SIZE), lambda g, m, p: (0, g)),
        ],
    )
    dk, dv = pl.pallas_call(
        attention_body,
        grid_spec=grid_spec,
        out_shape=[jax.ShapeDtypeStruct((window_rows, cols), jnp.float32)] * 2,
        compiler_params=pltpu.CompilerParams(dimension_semantics=("arbitrary", "arbitrary")),
    )(position.reshape(1).astype(jnp.int32), queries, out_grad, keys, values)
    return dk * scale, dv


def on_device(
    file_lengths,
    queries,
    out_grad,
    mem_key,
    memory_values,
    enc_rows,
    key_down,
    key_up,
    value_down,
    value_up,
):
    wide_count = lax.axis_size("wide")
    narrow_count = lax.axis_size("narrow")
    span = 8
    rows = mem_key.shape[0]
    cols = mem_key.shape[1]
    local_heads = cols // HEAD_SIZE
    stretch = lax.axis_index("wide")
    starts = jnp.cumsum(file_lengths) - file_lengths
    first = jnp.max(jnp.where(starts <= stretch, starts, 0))
    position = stretch - first
    window = jnp.stack([mem_key, memory_values])[None]
    reach = 1
    while reach < span:
        window = jnp.concatenate([window, passed_along(window, "wide", reach)], 0)
        reach *= 2
    keys = window[:, 0].reshape(span * rows, cols)
    values = window[:, 1].reshape(span * rows, cols)
    dkey, dval = attention_grads(position, queries, out_grad, keys, values)
    contrib = jnp.stack([dkey.reshape(span, rows, cols), dval.reshape(span, rows, cols)], 1)
    reach = span // 2
    while reach >= 1:
        sent = passed_along(contrib[reach : 2 * reach].astype(jnp.bfloat16), "wide", -reach)
        contrib = contrib[:reach] + sent.astype(jnp.float32)
        reach //= 2
    total = contrib[0]
    key_grad = total[0].astype(jnp.bfloat16)
    value_grad = total[1].astype(jnp.bfloat16)
    u_key = jnp.dot(enc_rows, key_down, preferred_element_type=jnp.float32).astype(jnp.bfloat16)
    u_value = jnp.dot(enc_rows, value_down, preferred_element_type=jnp.float32).astype(jnp.bfloat16)
    part_key = jnp.dot(key_grad, key_up.T, preferred_element_type=jnp.float32)
    part_value = jnp.dot(value_grad, value_up.T, preferred_element_type=jnp.float32)
    rank = part_key.shape[1]
    piece = rank // narrow_count
    parts = jnp.concatenate(
        [
            part_key.reshape(rows, narrow_count, piece).transpose(1, 0, 2),
            part_value.reshape(rows, narrow_count, piece).transpose(1, 0, 2),
        ],
        2,
    )
    h_both = scattered_sum(parts, "narrow").astype(jnp.bfloat16)
    up_key = jnp.dot(u_key.T, key_grad, preferred_element_type=jnp.float32)
    up_value = jnp.dot(u_value.T, value_grad, preferred_element_type=jnp.float32)
    down = jnp.dot(enc_rows.T, h_both, preferred_element_type=jnp.float32)
    width = down.shape[0] // wide_count
    up_both = jnp.stack([up_key, up_value]).reshape(wide_count, -1)
    joined = jnp.concatenate([down.reshape(wide_count, width * 2 * piece), up_both], 1)
    joined = scattered_sum(joined, "wide")
    down = joined[: width * 2 * piece].reshape(width, 2, piece)
    up_both = gathered(joined[width * 2 * piece :], "wide").reshape(2, rank, cols)
    down = gathered(down, "narrow").transpose(1, 2, 0, 3).reshape(width, 2, rank)
    return (down[:, 0], down[:, 1], up_both[0], up_both[1])


def solution(mesh):
    placed = (
        P(),
        P("wide", "narrow"),
        P("wide", "narrow"),
        P("wide", "narrow"),
        P("wide", "narrow"),
        P("wide", None),
        P(),
        P(None, "narrow"),
        P(),
        P(None, "narrow"),
    )
    return jax.shard_map(
        on_device,
        mesh=mesh,
        in_specs=placed,
        out_specs=(P("wide", None), P("wide", None), P(None, "narrow"), P(None, "narrow")),
        check_vma=False,
    )
```

```python
import jax
import jax.numpy as jnp
from jax import lax
from jax.experimental import pallas as pl
from jax.experimental.pallas import tpu as pltpu
from jax.sharding import PartitionSpec as P

HEAD_SIZE = 128
Q_PER_KV = 4


def passed_along(array, axis, by):
    devices = lax.axis_size(axis)
    pairs = [(i, i + by) for i in range(devices) if 0 <= i + by < devices]
    return lax.ppermute(array, axis, pairs)


def digit_steps(devices):
    steps = []
    low = 1
    while low < devices:
        radix = 4 if devices % (low * 4) == 0 else 2
        steps.append((low, radix))
        low *= radix
    return steps


def xor_partner(array, axis, mask):
    devices = lax.axis_size(axis)
    return lax.ppermute(array, axis, [(i, i ^ mask) for i in range(devices)])


def scattered_sum(x, axis):
    me = lax.axis_index(axis)
    for low, radix in digit_steps(lax.axis_size(axis)):
        group = x.reshape(x.shape[0] // radix, radix, *x.shape[1:])
        mine = (me // low) % radix
        x = lax.dynamic_index_in_dim(group, mine, axis=1, keepdims=False)
        for t in range(1, radix):
            give = lax.dynamic_index_in_dim(group, jnp.bitwise_xor(mine, t), axis=1, keepdims=False)
            x = x + xor_partner(give, axis, t * low)
    return x[0]


def gathered(y, axis):
    me = lax.axis_index(axis)
    y = y[None]
    for low, radix in reversed(digit_steps(lax.axis_size(axis))):
        mine = (me // low) % radix
        got = [y] + [xor_partner(y, axis, t * low) for t in range(1, radix)]
        order = jnp.bitwise_xor(jnp.arange(radix, dtype=mine.dtype), mine)
        y = jnp.take(jnp.stack(got, 1), order, axis=1)
        y = y.reshape(y.shape[0] * radix, *y.shape[2:])
    return y


def attention_body(pos_ref, q_ref, do_ref, k_ref, v_ref, dk_ref, dv_ref):
    m = pl.program_id(1)
    scale = HEAD_SIZE ** (-0.5)
    q = q_ref[...]
    do = do_ref[...]
    k = k_ref[...]
    v = v_ref[...]
    s = lax.dot_general(q, k, (((1,), (1,)), ((), ())), preferred_element_type=jnp.float32) * scale
    block = lax.broadcasted_iota(jnp.int32, s.shape, 1) // 128
    mask = block <= pos_ref[0]
    expo = jnp.where(mask, jnp.exp(jnp.where(mask, s, 0.0)), 0.0)
    prob = expo / jnp.sum(expo, axis=-1, keepdims=True)
    prob_b = prob.astype(jnp.bfloat16)
    outp = jnp.dot(prob_b, v, preferred_element_type=jnp.float32)
    delta = jnp.sum(do.astype(jnp.float32) * outp, axis=-1, keepdims=True)
    dprob = lax.dot_general(do, v, (((1,), (1,)), ((), ())), preferred_element_type=jnp.float32)
    dscore = (prob * (dprob - delta)).astype(jnp.bfloat16)
    dk = lax.dot_general(dscore, q, (((0,), (0,)), ((), ())), preferred_element_type=jnp.float32)
    dv = lax.dot_general(prob_b, do, (((0,), (0,)), ((), ())), preferred_element_type=jnp.float32)

    @pl.when(m == 0)
    def _():
        dk_ref[...] = dk
        dv_ref[...] = dv

    @pl.when(m > 0)
    def _():
        dk_ref[...] += dk
        dv_ref[...] += dv


def attention_grads(position, queries, out_grad, keys, values):
    tokens = queries.shape[0]
    window_rows, cols = keys.shape
    heads = cols // HEAD_SIZE
    scale = HEAD_SIZE ** (-0.5)
    grid_spec = pltpu.PrefetchScalarGridSpec(
        num_scalar_prefetch=1,
        grid=(heads, Q_PER_KV),
        in_specs=[
            pl.BlockSpec((tokens, HEAD_SIZE), lambda g, m, p: (0, g * Q_PER_KV + m)),
            pl.BlockSpec((tokens, HEAD_SIZE), lambda g, m, p: (0, g * Q_PER_KV + m)),
            pl.BlockSpec((window_rows, HEAD_SIZE), lambda g, m, p: (0, g)),
            pl.BlockSpec((window_rows, HEAD_SIZE), lambda g, m, p: (0, g)),
        ],
        out_specs=[
            pl.BlockSpec((window_rows, HEAD_SIZE), lambda g, m, p: (0, g)),
            pl.BlockSpec((window_rows, HEAD_SIZE), lambda g, m, p: (0, g)),
        ],
    )
    dk, dv = pl.pallas_call(
        attention_body,
        grid_spec=grid_spec,
        out_shape=[jax.ShapeDtypeStruct((window_rows, cols), jnp.float32)] * 2,
        compiler_params=pltpu.CompilerParams(dimension_semantics=("arbitrary", "arbitrary")),
    )(position.reshape(1).astype(jnp.int32), queries, out_grad, keys, values)
    return dk * scale, dv


def on_device(
    file_lengths,
    queries,
    out_grad,
    mem_key,
    memory_values,
    enc_rows,
    key_down,
    key_up,
    value_down,
    value_up,
):
    wide_count = lax.axis_size("wide")
    narrow_count = lax.axis_size("narrow")
    span = 8
    rows = mem_key.shape[0]
    cols = mem_key.shape[1]
    local_heads = cols // HEAD_SIZE
    stretch = lax.axis_index("wide")
    starts = jnp.cumsum(file_lengths) - file_lengths
    first = jnp.max(jnp.where(starts <= stretch, starts, 0))
    position = stretch - first
    window = jnp.stack([mem_key, memory_values])[None]
    reach = 1
    while reach < span:
        window = jnp.concatenate([window, passed_along(window, "wide", reach)], 0)
        reach *= 2
    keys = window[:, 0].reshape(span * rows, cols)
    values = window[:, 1].reshape(span * rows, cols)
    dkey, dval = attention_grads(position, queries, out_grad, keys, values)
    contrib = jnp.stack([dkey.reshape(span, rows, cols), dval.reshape(span, rows, cols)], 1)
    reach = span // 2
    while reach >= 1:
        give = contrib[reach : 2 * reach]
        if reach == span // 2:
            give = give.astype(jnp.bfloat16)
        contrib = contrib[:reach] + passed_along(give, "wide", -reach).astype(jnp.float32)
        reach //= 2
    total = contrib[0]
    key_grad = total[0].astype(jnp.bfloat16)
    value_grad = total[1].astype(jnp.bfloat16)
    u_key = jnp.dot(enc_rows, key_down, preferred_element_type=jnp.float32).astype(jnp.bfloat16)
    u_value = jnp.dot(enc_rows, value_down, preferred_element_type=jnp.float32).astype(jnp.bfloat16)
    part_key = jnp.dot(key_grad, key_up.T, preferred_element_type=jnp.float32)
    part_value = jnp.dot(value_grad, value_up.T, preferred_element_type=jnp.float32)
    rank = part_key.shape[1]
    piece = rank // narrow_count
    parts = jnp.concatenate(
        [
            part_key.reshape(rows, narrow_count, piece).transpose(1, 0, 2),
            part_value.reshape(rows, narrow_count, piece).transpose(1, 0, 2),
        ],
        2,
    )
    h_both = scattered_sum(parts, "narrow").astype(jnp.bfloat16)
    up_key = jnp.dot(u_key.T, key_grad, preferred_element_type=jnp.float32)
    up_value = jnp.dot(u_value.T, value_grad, preferred_element_type=jnp.float32)
    down = jnp.dot(enc_rows.T, h_both, preferred_element_type=jnp.float32)
    width = down.shape[0] // wide_count
    up_both = jnp.stack([up_key, up_value]).reshape(wide_count, -1)
    joined = jnp.concatenate([down.reshape(wide_count, width * 2 * piece), up_both], 1)
    joined = scattered_sum(joined, "wide")
    down = joined[: width * 2 * piece].reshape(width, 2, piece)
    up_both = gathered(joined[width * 2 * piece :], "wide").reshape(2, rank, cols)
    down = gathered(down, "narrow").transpose(1, 2, 0, 3).reshape(width, 2, rank)
    return (down[:, 0], down[:, 1], up_both[0], up_both[1])


def solution(mesh):
    placed = (
        P(),
        P("wide", "narrow"),
        P("wide", "narrow"),
        P("wide", "narrow"),
        P("wide", "narrow"),
        P("wide", None),
        P(),
        P(None, "narrow"),
        P(),
        P(None, "narrow"),
    )
    return jax.shard_map(
        on_device,
        mesh=mesh,
        in_specs=placed,
        out_specs=(P("wide", None), P("wide", None), P(None, "narrow"), P(None, "narrow")),
        check_vma=False,
    )
```

```python
import jax
import jax.numpy as jnp
from jax import lax
from jax.experimental import pallas as pl
from jax.experimental.pallas import tpu as pltpu
from jax.sharding import PartitionSpec as P

HEAD_SIZE = 128
Q_PER_KV = 4


def passed_along(array, axis, by):
    devices = lax.axis_size(axis)
    pairs = [(i, i + by) for i in range(devices) if 0 <= i + by < devices]
    return lax.ppermute(array, axis, pairs)


def digit_steps(devices):
    steps = []
    low = 1
    while low < devices:
        radix = 4 if devices % (low * 4) == 0 else 2
        steps.append((low, radix))
        low *= radix
    return steps


def xor_partner(array, axis, mask):
    devices = lax.axis_size(axis)
    return lax.ppermute(array, axis, [(i, i ^ mask) for i in range(devices)])


def scattered_sum(x, axis):
    me = lax.axis_index(axis)
    for low, radix in digit_steps(lax.axis_size(axis)):
        group = x.reshape(x.shape[0] // radix, radix, *x.shape[1:])
        mine = (me // low) % radix
        x = lax.dynamic_index_in_dim(group, mine, axis=1, keepdims=False)
        for t in range(1, radix):
            give = lax.dynamic_index_in_dim(group, jnp.bitwise_xor(mine, t), axis=1, keepdims=False)
            x = x + xor_partner(give, axis, t * low)
    return x[0]


def gathered(y, axis):
    me = lax.axis_index(axis)
    y = y[None]
    for low, radix in reversed(digit_steps(lax.axis_size(axis))):
        mine = (me // low) % radix
        got = [y] + [xor_partner(y, axis, t * low) for t in range(1, radix)]
        order = jnp.bitwise_xor(jnp.arange(radix, dtype=mine.dtype), mine)
        y = jnp.take(jnp.stack(got, 1), order, axis=1)
        y = y.reshape(y.shape[0] * radix, *y.shape[2:])
    return y


def attention_body(pos_ref, q_ref, do_ref, k_ref, v_ref, dk_ref, dv_ref):
    m = pl.program_id(1)
    scale = HEAD_SIZE ** (-0.5)
    q = q_ref[...]
    do = do_ref[...]
    k = k_ref[...]
    v = v_ref[...]
    s = lax.dot_general(q, k, (((1,), (1,)), ((), ())), preferred_element_type=jnp.float32) * scale
    block = lax.broadcasted_iota(jnp.int32, (1, s.shape[1]), 1) // 128
    expo = jnp.exp(jnp.where(block <= pos_ref[0], s, -jnp.inf))
    prob = expo * (1.0 / jnp.sum(expo, axis=-1, keepdims=True))
    prob_b = prob.astype(jnp.bfloat16)
    outp = jnp.dot(prob_b, v, preferred_element_type=jnp.float32)
    delta = jnp.sum(do.astype(jnp.float32) * outp, axis=-1, keepdims=True)
    dprob = lax.dot_general(do, v, (((1,), (1,)), ((), ())), preferred_element_type=jnp.float32)
    dscore = (prob * (dprob - delta)).astype(jnp.bfloat16)
    dk = lax.dot_general(dscore, q, (((0,), (0,)), ((), ())), preferred_element_type=jnp.float32)
    dv = lax.dot_general(prob_b, do, (((0,), (0,)), ((), ())), preferred_element_type=jnp.float32)

    @pl.when(m == 0)
    def _():
        dk_ref[...] = dk
        dv_ref[...] = dv

    @pl.when(m > 0)
    def _():
        dk_ref[...] += dk
        dv_ref[...] += dv


def attention_grads(position, queries, out_grad, keys, values):
    tokens = queries.shape[0]
    window_rows, cols = keys.shape
    heads = cols // HEAD_SIZE
    scale = HEAD_SIZE ** (-0.5)
    grid_spec = pltpu.PrefetchScalarGridSpec(
        num_scalar_prefetch=1,
        grid=(heads, Q_PER_KV),
        in_specs=[
            pl.BlockSpec((tokens, HEAD_SIZE), lambda g, m, p: (0, g * Q_PER_KV + m)),
            pl.BlockSpec((tokens, HEAD_SIZE), lambda g, m, p: (0, g * Q_PER_KV + m)),
            pl.BlockSpec((window_rows, HEAD_SIZE), lambda g, m, p: (0, g)),
            pl.BlockSpec((window_rows, HEAD_SIZE), lambda g, m, p: (0, g)),
        ],
        out_specs=[
            pl.BlockSpec((window_rows, HEAD_SIZE), lambda g, m, p: (0, g)),
            pl.BlockSpec((window_rows, HEAD_SIZE), lambda g, m, p: (0, g)),
        ],
    )
    dk, dv = pl.pallas_call(
        attention_body,
        grid_spec=grid_spec,
        out_shape=[jax.ShapeDtypeStruct((window_rows, cols), jnp.float32)] * 2,
        compiler_params=pltpu.CompilerParams(dimension_semantics=("arbitrary", "arbitrary")),
    )(position.reshape(1).astype(jnp.int32), queries, out_grad, keys, values)
    return dk * scale, dv


def on_device(
    file_lengths,
    queries,
    out_grad,
    mem_key,
    memory_values,
    enc_rows,
    key_down,
    key_up,
    value_down,
    value_up,
):
    wide_count = lax.axis_size("wide")
    narrow_count = lax.axis_size("narrow")
    span = 8
    rows = mem_key.shape[0]
    cols = mem_key.shape[1]
    local_heads = cols // HEAD_SIZE
    stretch = lax.axis_index("wide")
    starts = jnp.cumsum(file_lengths) - file_lengths
    first = jnp.max(jnp.where(starts <= stretch, starts, 0))
    position = stretch - first
    window = jnp.stack([mem_key, memory_values])[None]
    reach = 1
    while reach < span:
        window = jnp.concatenate([window, passed_along(window, "wide", reach)], 0)
        reach *= 2
    keys = window[:, 0].reshape(span * rows, cols)
    values = window[:, 1].reshape(span * rows, cols)
    dkey, dval = attention_grads(position, queries, out_grad, keys, values)
    contrib = jnp.stack([dkey.reshape(span, rows, cols), dval.reshape(span, rows, cols)], 1)
    reach = span // 2
    while reach >= 1:
        give = contrib[reach : 2 * reach]
        if reach == span // 2:
            give = give.astype(jnp.bfloat16)
        contrib = contrib[:reach] + passed_along(give, "wide", -reach).astype(jnp.float32)
        reach //= 2
    total = contrib[0]
    key_grad = total[0].astype(jnp.bfloat16)
    value_grad = total[1].astype(jnp.bfloat16)
    u_key = jnp.dot(enc_rows, key_down, preferred_element_type=jnp.float32).astype(jnp.bfloat16)
    u_value = jnp.dot(enc_rows, value_down, preferred_element_type=jnp.float32).astype(jnp.bfloat16)
    part_key = jnp.dot(key_grad, key_up.T, preferred_element_type=jnp.float32)
    part_value = jnp.dot(value_grad, value_up.T, preferred_element_type=jnp.float32)
    rank = part_key.shape[1]
    piece = rank // narrow_count
    parts = jnp.concatenate(
        [
            part_key.reshape(rows, narrow_count, piece).transpose(1, 0, 2),
            part_value.reshape(rows, narrow_count, piece).transpose(1, 0, 2),
        ],
        2,
    )
    h_both = scattered_sum(parts, "narrow").astype(jnp.bfloat16)
    up_key = jnp.dot(u_key.T, key_grad, preferred_element_type=jnp.float32)
    up_value = jnp.dot(u_value.T, value_grad, preferred_element_type=jnp.float32)
    down = jnp.dot(enc_rows.T, h_both, preferred_element_type=jnp.float32)
    width = down.shape[0] // wide_count
    up_both = jnp.stack([up_key, up_value]).reshape(wide_count, -1)
    joined = jnp.concatenate([down.reshape(wide_count, width * 2 * piece), up_both], 1)
    joined = scattered_sum(joined, "wide")
    down = joined[: width * 2 * piece].reshape(width, 2, piece)
    up_both = gathered(joined[width * 2 * piece :], "wide").reshape(2, rank, cols)
    down = gathered(down, "narrow").transpose(1, 2, 0, 3).reshape(width, 2, rank)
    return (down[:, 0], down[:, 1], up_both[0], up_both[1])


def solution(mesh):
    placed = (
        P(),
        P("wide", "narrow"),
        P("wide", "narrow"),
        P("wide", "narrow"),
        P("wide", "narrow"),
        P("wide", None),
        P(),
        P(None, "narrow"),
        P(),
        P(None, "narrow"),
    )
    return jax.shard_map(
        on_device,
        mesh=mesh,
        in_specs=placed,
        out_specs=(P("wide", None), P("wide", None), P(None, "narrow"), P(None, "narrow")),
        check_vma=False,
    )
```

```python
import jax
import jax.numpy as jnp
from jax import lax
from jax.experimental import pallas as pl
from jax.experimental.pallas import tpu as pltpu
from jax.sharding import PartitionSpec as P

HEAD_SIZE = 128
Q_PER_KV = 4


def passed_along(array, axis, by):
    devices = lax.axis_size(axis)
    pairs = [(i, i + by) for i in range(devices) if 0 <= i + by < devices]
    return lax.ppermute(array, axis, pairs)


def digit_steps(devices):
    steps = []
    low = 1
    while low < devices:
        radix = 4 if devices % (low * 4) == 0 else 2
        steps.append((low, radix))
        low *= radix
    return steps


def xor_partner(array, axis, mask):
    devices = lax.axis_size(axis)
    return lax.ppermute(array, axis, [(i, i ^ mask) for i in range(devices)])


def scattered_sum(x, axis, first_kind=None):
    me = lax.axis_index(axis)
    for step, (low, radix) in enumerate(digit_steps(lax.axis_size(axis))):
        group = x.reshape(x.shape[0] // radix, radix, *x.shape[1:])
        mine = (me // low) % radix
        x = lax.dynamic_index_in_dim(group, mine, axis=1, keepdims=False)
        for t in range(1, radix):
            give = lax.dynamic_index_in_dim(group, jnp.bitwise_xor(mine, t), axis=1, keepdims=False)
            if step == 0 and first_kind is not None:
                give = give.astype(first_kind)
            x = x + xor_partner(give, axis, t * low).astype(x.dtype)
    return x[0]


def gathered(y, axis):
    me = lax.axis_index(axis)
    y = y[None]
    for low, radix in reversed(digit_steps(lax.axis_size(axis))):
        mine = (me // low) % radix
        got = [y] + [xor_partner(y, axis, t * low) for t in range(1, radix)]
        order = jnp.bitwise_xor(jnp.arange(radix, dtype=mine.dtype), mine)
        y = jnp.take(jnp.stack(got, 1), order, axis=1)
        y = y.reshape(y.shape[0] * radix, *y.shape[2:])
    return y


def attention_body(pos_ref, q_ref, do_ref, k_ref, v_ref, dk_ref, dv_ref):
    m = pl.program_id(1)
    scale = HEAD_SIZE ** (-0.5)
    q = q_ref[...]
    do = do_ref[...]
    k = k_ref[...]
    v = v_ref[...]
    s = lax.dot_general(q, k, (((1,), (1,)), ((), ())), preferred_element_type=jnp.float32) * scale
    block = lax.broadcasted_iota(jnp.int32, (1, s.shape[1]), 1) // 128
    expo = jnp.exp(jnp.where(block <= pos_ref[0], s, -jnp.inf))
    prob = expo * (1.0 / jnp.sum(expo, axis=-1, keepdims=True))
    prob_b = prob.astype(jnp.bfloat16)
    outp = jnp.dot(prob_b, v, preferred_element_type=jnp.float32)
    delta = jnp.sum(do.astype(jnp.float32) * outp, axis=-1, keepdims=True)
    dprob = lax.dot_general(do, v, (((1,), (1,)), ((), ())), preferred_element_type=jnp.float32)
    dscore = (prob * (dprob - delta)).astype(jnp.bfloat16)
    dk = lax.dot_general(dscore, q, (((0,), (0,)), ((), ())), preferred_element_type=jnp.float32)
    dv = lax.dot_general(prob_b, do, (((0,), (0,)), ((), ())), preferred_element_type=jnp.float32)

    @pl.when(m == 0)
    def _():
        dk_ref[...] = dk
        dv_ref[...] = dv

    @pl.when(m > 0)
    def _():
        dk_ref[...] += dk
        dv_ref[...] += dv


def attention_grads(position, queries, out_grad, keys, values):
    tokens = queries.shape[0]
    window_rows, cols = keys.shape
    heads = cols // HEAD_SIZE
    scale = HEAD_SIZE ** (-0.5)
    grid_spec = pltpu.PrefetchScalarGridSpec(
        num_scalar_prefetch=1,
        grid=(heads, Q_PER_KV),
        in_specs=[
            pl.BlockSpec((tokens, HEAD_SIZE), lambda g, m, p: (0, g * Q_PER_KV + m)),
            pl.BlockSpec((tokens, HEAD_SIZE), lambda g, m, p: (0, g * Q_PER_KV + m)),
            pl.BlockSpec((window_rows, HEAD_SIZE), lambda g, m, p: (0, g)),
            pl.BlockSpec((window_rows, HEAD_SIZE), lambda g, m, p: (0, g)),
        ],
        out_specs=[
            pl.BlockSpec((window_rows, HEAD_SIZE), lambda g, m, p: (0, g)),
            pl.BlockSpec((window_rows, HEAD_SIZE), lambda g, m, p: (0, g)),
        ],
    )
    dk, dv = pl.pallas_call(
        attention_body,
        grid_spec=grid_spec,
        out_shape=[jax.ShapeDtypeStruct((window_rows, cols), jnp.float32)] * 2,
        compiler_params=pltpu.CompilerParams(dimension_semantics=("arbitrary", "arbitrary")),
    )(position.reshape(1).astype(jnp.int32), queries, out_grad, keys, values)
    return dk * scale, dv


def on_device(
    file_lengths,
    queries,
    out_grad,
    mem_key,
    memory_values,
    enc_rows,
    key_down,
    key_up,
    value_down,
    value_up,
):
    wide_count = lax.axis_size("wide")
    narrow_count = lax.axis_size("narrow")
    span = 8
    rows = mem_key.shape[0]
    cols = mem_key.shape[1]
    local_heads = cols // HEAD_SIZE
    stretch = lax.axis_index("wide")
    starts = jnp.cumsum(file_lengths) - file_lengths
    first = jnp.max(jnp.where(starts <= stretch, starts, 0))
    position = stretch - first
    window = jnp.stack([mem_key, memory_values])[None]
    reach = 1
    while reach < span:
        window = jnp.concatenate([window, passed_along(window, "wide", reach)], 0)
        reach *= 2
    keys = window[:, 0].reshape(span * rows, cols)
    values = window[:, 1].reshape(span * rows, cols)
    dkey, dval = attention_grads(position, queries, out_grad, keys, values)
    contrib = jnp.stack([dkey.reshape(span, rows, cols), dval.reshape(span, rows, cols)], 1)
    reach = span // 2
    while reach >= 1:
        give = contrib[reach : 2 * reach]
        if reach == span // 2:
            give = give.astype(jnp.bfloat16)
        contrib = contrib[:reach] + passed_along(give, "wide", -reach).astype(jnp.float32)
        reach //= 2
    total = contrib[0]
    key_grad = total[0].astype(jnp.bfloat16)
    value_grad = total[1].astype(jnp.bfloat16)
    u_key = jnp.dot(enc_rows, key_down, preferred_element_type=jnp.float32).astype(jnp.bfloat16)
    u_value = jnp.dot(enc_rows, value_down, preferred_element_type=jnp.float32).astype(jnp.bfloat16)
    part_key = jnp.dot(key_grad, key_up.T, preferred_element_type=jnp.float32)
    part_value = jnp.dot(value_grad, value_up.T, preferred_element_type=jnp.float32)
    rank = part_key.shape[1]
    piece = rank // narrow_count
    parts = jnp.concatenate(
        [
            part_key.reshape(rows, narrow_count, piece).transpose(1, 0, 2),
            part_value.reshape(rows, narrow_count, piece).transpose(1, 0, 2),
        ],
        2,
    )
    h_both = scattered_sum(parts, "narrow").astype(jnp.bfloat16)
    up_key = jnp.dot(u_key.T, key_grad, preferred_element_type=jnp.float32)
    up_value = jnp.dot(u_value.T, value_grad, preferred_element_type=jnp.float32)
    down = jnp.dot(enc_rows.T, h_both, preferred_element_type=jnp.float32)
    width = down.shape[0] // wide_count
    up_both = jnp.stack([up_key, up_value]).reshape(wide_count, -1)
    joined = jnp.concatenate([down.reshape(wide_count, width * 2 * piece), up_both], 1)
    joined = scattered_sum(joined, "wide", jnp.bfloat16)
    down = joined[: width * 2 * piece].reshape(width, 2, piece)
    up_both = gathered(joined[width * 2 * piece :], "wide").reshape(2, rank, cols)
    down = gathered(down, "narrow").transpose(1, 2, 0, 3).reshape(width, 2, rank)
    return (down[:, 0], down[:, 1], up_both[0], up_both[1])


def solution(mesh):
    placed = (
        P(),
        P("wide", "narrow"),
        P("wide", "narrow"),
        P("wide", "narrow"),
        P("wide", "narrow"),
        P("wide", None),
        P(),
        P(None, "narrow"),
        P(),
        P(None, "narrow"),
    )
    return jax.shard_map(
        on_device,
        mesh=mesh,
        in_specs=placed,
        out_specs=(P("wide", None), P("wide", None), P(None, "narrow"), P(None, "narrow")),
        check_vma=False,
    )
```

```python
import jax
import jax.numpy as jnp
from jax import lax
from jax.experimental import pallas as pl
from jax.experimental.pallas import tpu as pltpu
from jax.sharding import PartitionSpec as P

HEAD_SIZE = 128
Q_PER_KV = 4


def passed_along(array, axis, by):
    devices = lax.axis_size(axis)
    pairs = [(i, i + by) for i in range(devices) if 0 <= i + by < devices]
    return lax.ppermute(array, axis, pairs)


def digit_steps(devices):
    steps = []
    low = 1
    while low < devices:
        radix = 4 if devices % (low * 4) == 0 else 2
        steps.append((low, radix))
        low *= radix
    return steps


def xor_partner(array, axis, mask):
    devices = lax.axis_size(axis)
    return lax.ppermute(array, axis, [(i, i ^ mask) for i in range(devices)])


def scattered_sum(x, axis, first_kind=None):
    me = lax.axis_index(axis)
    for step, (low, radix) in enumerate(digit_steps(lax.axis_size(axis))):
        group = x.reshape(x.shape[0] // radix, radix, *x.shape[1:])
        mine = (me // low) % radix
        x = lax.dynamic_index_in_dim(group, mine, axis=1, keepdims=False)
        for t in range(1, radix):
            give = lax.dynamic_index_in_dim(group, jnp.bitwise_xor(mine, t), axis=1, keepdims=False)
            if step == 0 and first_kind is not None:
                give = give.astype(first_kind)
            x = x + xor_partner(give, axis, t * low).astype(x.dtype)
    return x[0]


def wide_sums(parted, whole, axis):
    me = lax.axis_index(axis)
    steps = digit_steps(lax.axis_size(axis))
    low, radix = steps[0]
    split = parted.shape[1]
    x = jnp.concatenate([parted, whole], 1)
    group = x.reshape(x.shape[0] // radix, radix, *x.shape[1:])
    first = (me // low) % radix
    x = lax.dynamic_index_in_dim(group, first, axis=1, keepdims=False)
    for t in range(1, radix):
        give = lax.dynamic_index_in_dim(group, jnp.bitwise_xor(first, t), axis=1, keepdims=False)
        x = x + xor_partner(give.astype(jnp.bfloat16), axis, t * low).astype(x.dtype)
    parted = x[:, :split]
    whole = x[:, split:]
    for low, radix in steps[1:]:
        group = parted.reshape(parted.shape[0] // radix, radix, *parted.shape[1:])
        mine = (me // low) % radix
        parted = lax.dynamic_index_in_dim(group, mine, axis=1, keepdims=False)
        size = parted.size
        wholes = [whole]
        for t in range(1, radix):
            give = lax.dynamic_index_in_dim(group, jnp.bitwise_xor(mine, t), axis=1, keepdims=False)
            back = xor_partner(jnp.concatenate([give.reshape(-1), whole.reshape(-1)]), axis, t * low)
            parted = parted + back[:size].reshape(parted.shape)
            wholes.append(back[size:].reshape(whole.shape))
        order = jnp.bitwise_xor(jnp.arange(radix, dtype=mine.dtype), mine)
        ranked = jnp.take(jnp.stack(wholes), order, axis=0)
        whole = ranked[0]
        for d in range(1, radix):
            whole = whole + ranked[d]
    low, radix = steps[0]
    got = [whole] + [xor_partner(whole, axis, t * low) for t in range(1, radix)]
    order = jnp.bitwise_xor(jnp.arange(radix, dtype=first.dtype), first)
    whole = jnp.take(jnp.stack(got, 1), order, axis=1)
    whole = whole.reshape(whole.shape[0] * radix, *whole.shape[2:])
    return parted[0], whole


def gathered(y, axis):
    me = lax.axis_index(axis)
    y = y[None]
    for low, radix in reversed(digit_steps(lax.axis_size(axis))):
        mine = (me // low) % radix
        got = [y] + [xor_partner(y, axis, t * low) for t in range(1, radix)]
        order = jnp.bitwise_xor(jnp.arange(radix, dtype=mine.dtype), mine)
        y = jnp.take(jnp.stack(got, 1), order, axis=1)
        y = y.reshape(y.shape[0] * radix, *y.shape[2:])
    return y


def attention_body(pos_ref, q_ref, do_ref, k_ref, v_ref, dk_ref, dv_ref):
    m = pl.program_id(1)
    scale = HEAD_SIZE ** (-0.5)
    q = q_ref[...]
    do = do_ref[...]
    k = k_ref[...]
    v = v_ref[...]
    s = lax.dot_general(q, k, (((1,), (1,)), ((), ())), preferred_element_type=jnp.float32) * scale
    block = lax.broadcasted_iota(jnp.int32, (1, s.shape[1]), 1) // 128
    expo = jnp.exp(jnp.where(block <= pos_ref[0], s, -jnp.inf))
    prob = expo * (1.0 / jnp.sum(expo, axis=-1, keepdims=True))
    prob_b = prob.astype(jnp.bfloat16)
    outp = jnp.dot(prob_b, v, preferred_element_type=jnp.float32)
    delta = jnp.sum(do.astype(jnp.float32) * outp, axis=-1, keepdims=True)
    dprob = lax.dot_general(do, v, (((1,), (1,)), ((), ())), preferred_element_type=jnp.float32)
    dscore = (prob * (dprob - delta)).astype(jnp.bfloat16)
    dk = lax.dot_general(dscore, q, (((0,), (0,)), ((), ())), preferred_element_type=jnp.float32)
    dv = lax.dot_general(prob_b, do, (((0,), (0,)), ((), ())), preferred_element_type=jnp.float32)

    @pl.when(m == 0)
    def _():
        dk_ref[...] = dk
        dv_ref[...] = dv

    @pl.when(m > 0)
    def _():
        dk_ref[...] += dk
        dv_ref[...] += dv


def attention_grads(position, queries, out_grad, keys, values):
    tokens = queries.shape[0]
    window_rows, cols = keys.shape
    heads = cols // HEAD_SIZE
    scale = HEAD_SIZE ** (-0.5)
    grid_spec = pltpu.PrefetchScalarGridSpec(
        num_scalar_prefetch=1,
        grid=(heads, Q_PER_KV),
        in_specs=[
            pl.BlockSpec((tokens, HEAD_SIZE), lambda g, m, p: (0, g * Q_PER_KV + m)),
            pl.BlockSpec((tokens, HEAD_SIZE), lambda g, m, p: (0, g * Q_PER_KV + m)),
            pl.BlockSpec((window_rows, HEAD_SIZE), lambda g, m, p: (0, g)),
            pl.BlockSpec((window_rows, HEAD_SIZE), lambda g, m, p: (0, g)),
        ],
        out_specs=[
            pl.BlockSpec((window_rows, HEAD_SIZE), lambda g, m, p: (0, g)),
            pl.BlockSpec((window_rows, HEAD_SIZE), lambda g, m, p: (0, g)),
        ],
    )
    dk, dv = pl.pallas_call(
        attention_body,
        grid_spec=grid_spec,
        out_shape=[jax.ShapeDtypeStruct((window_rows, cols), jnp.float32)] * 2,
        compiler_params=pltpu.CompilerParams(dimension_semantics=("arbitrary", "arbitrary")),
    )(position.reshape(1).astype(jnp.int32), queries, out_grad, keys, values)
    return dk * scale, dv


def on_device(
    file_lengths,
    queries,
    out_grad,
    mem_key,
    memory_values,
    enc_rows,
    key_down,
    key_up,
    value_down,
    value_up,
):
    wide_count = lax.axis_size("wide")
    narrow_count = lax.axis_size("narrow")
    span = 8
    rows = mem_key.shape[0]
    cols = mem_key.shape[1]
    local_heads = cols // HEAD_SIZE
    stretch = lax.axis_index("wide")
    starts = jnp.cumsum(file_lengths) - file_lengths
    first = jnp.max(jnp.where(starts <= stretch, starts, 0))
    position = stretch - first
    window = jnp.stack([mem_key, memory_values])[None]
    reach = 1
    while reach < span:
        window = jnp.concatenate([window, passed_along(window, "wide", reach)], 0)
        reach *= 2
    keys = window[:, 0].reshape(span * rows, cols)
    values = window[:, 1].reshape(span * rows, cols)
    dkey, dval = attention_grads(position, queries, out_grad, keys, values)
    contrib = jnp.stack([dkey.reshape(span, rows, cols), dval.reshape(span, rows, cols)], 1)
    reach = span // 2
    while reach >= 1:
        give = contrib[reach : 2 * reach]
        if reach == span // 2:
            give = give.astype(jnp.bfloat16)
        contrib = contrib[:reach] + passed_along(give, "wide", -reach).astype(jnp.float32)
        reach //= 2
    total = contrib[0]
    key_grad = total[0].astype(jnp.bfloat16)
    value_grad = total[1].astype(jnp.bfloat16)
    u_key = jnp.dot(enc_rows, key_down, preferred_element_type=jnp.float32).astype(jnp.bfloat16)
    u_value = jnp.dot(enc_rows, value_down, preferred_element_type=jnp.float32).astype(jnp.bfloat16)
    part_key = jnp.dot(key_grad, key_up.T, preferred_element_type=jnp.float32)
    part_value = jnp.dot(value_grad, value_up.T, preferred_element_type=jnp.float32)
    rank = part_key.shape[1]
    piece = rank // narrow_count
    parts = jnp.concatenate(
        [
            part_key.reshape(rows, narrow_count, piece).transpose(1, 0, 2),
            part_value.reshape(rows, narrow_count, piece).transpose(1, 0, 2),
        ],
        2,
    )
    h_both = scattered_sum(parts, "narrow").astype(jnp.bfloat16)
    up_key = jnp.dot(u_key.T, key_grad, preferred_element_type=jnp.float32)
    up_value = jnp.dot(u_value.T, value_grad, preferred_element_type=jnp.float32)
    down = jnp.dot(enc_rows.T, h_both, preferred_element_type=jnp.float32)
    width = down.shape[0] // wide_count
    up_both = jnp.stack([up_key, up_value]).reshape(wide_count, -1)
    down, up_both = wide_sums(down.reshape(wide_count, width * 2 * piece), up_both, "wide")
    down = down.reshape(width, 2, piece)
    up_both = up_both.reshape(2, rank, cols)
    down = gathered(down, "narrow").transpose(1, 2, 0, 3).reshape(width, 2, rank)
    return (down[:, 0], down[:, 1], up_both[0], up_both[1])


def solution(mesh):
    placed = (
        P(),
        P("wide", "narrow"),
        P("wide", "narrow"),
        P("wide", "narrow"),
        P("wide", "narrow"),
        P("wide", None),
        P(),
        P(None, "narrow"),
        P(),
        P(None, "narrow"),
    )
    return jax.shard_map(
        on_device,
        mesh=mesh,
        in_specs=placed,
        out_specs=(P("wide", None), P("wide", None), P(None, "narrow"), P(None, "narrow")),
        check_vma=False,
    )
```

```python
import jax
import jax.numpy as jnp
from jax import lax
from jax.experimental import pallas as pl
from jax.experimental.pallas import tpu as pltpu
from jax.sharding import PartitionSpec as P

HEAD_SIZE = 128
Q_PER_KV = 4


def passed_along(array, axis, by):
    devices = lax.axis_size(axis)
    pairs = [(i, i + by) for i in range(devices) if 0 <= i + by < devices]
    return lax.ppermute(array, axis, pairs)


def digit_steps(devices):
    steps = []
    low = 1
    while low < devices:
        radix = 4 if devices % (low * 4) == 0 else 2
        steps.append((low, radix))
        low *= radix
    return steps


def xor_partner(array, axis, mask):
    devices = lax.axis_size(axis)
    return lax.ppermute(array, axis, [(i, i ^ mask) for i in range(devices)])


def scattered_sum(x, axis, first_kind=None):
    me = lax.axis_index(axis)
    for step, (low, radix) in enumerate(digit_steps(lax.axis_size(axis))):
        group = x.reshape(x.shape[0] // radix, radix, *x.shape[1:])
        mine = (me // low) % radix
        x = lax.dynamic_index_in_dim(group, mine, axis=1, keepdims=False)
        for t in range(1, radix):
            give = lax.dynamic_index_in_dim(group, jnp.bitwise_xor(mine, t), axis=1, keepdims=False)
            if step == 0 and first_kind is not None:
                give = give.astype(first_kind)
            x = x + xor_partner(give, axis, t * low).astype(x.dtype)
    return x[0]


def wide_sums(parted, whole, axis):
    me = lax.axis_index(axis)
    steps = digit_steps(lax.axis_size(axis))
    low, radix = steps[0]
    split = parted.shape[1]
    x = jnp.concatenate([parted, whole], 1)
    group = x.reshape(x.shape[0] // radix, radix, *x.shape[1:])
    first = (me // low) % radix
    x = lax.dynamic_index_in_dim(group, first, axis=1, keepdims=False)
    for t in range(1, radix):
        give = lax.dynamic_index_in_dim(group, jnp.bitwise_xor(first, t), axis=1, keepdims=False)
        x = x + xor_partner(give.astype(jnp.bfloat16), axis, t * low).astype(x.dtype)
    parted = x[:, :split]
    whole = x[:, split:]
    for low, radix in steps[1:]:
        group = parted.reshape(parted.shape[0] // radix, radix, *parted.shape[1:])
        mine = (me // low) % radix
        parted = lax.dynamic_index_in_dim(group, mine, axis=1, keepdims=False)
        size = parted.size
        wholes = [whole]
        for t in range(1, radix):
            give = lax.dynamic_index_in_dim(group, jnp.bitwise_xor(mine, t), axis=1, keepdims=False)
            back = xor_partner(jnp.concatenate([give.reshape(-1), whole.reshape(-1)]), axis, t * low)
            parted = parted + back[:size].reshape(parted.shape)
            wholes.append(back[size:].reshape(whole.shape))
        order = jnp.bitwise_xor(jnp.arange(radix, dtype=mine.dtype), mine)
        ranked = jnp.take(jnp.stack(wholes), order, axis=0)
        whole = ranked[0]
        for d in range(1, radix):
            whole = whole + ranked[d]
    low, radix = steps[0]
    got = [whole] + [xor_partner(whole, axis, t * low) for t in range(1, radix)]
    order = jnp.bitwise_xor(jnp.arange(radix, dtype=first.dtype), first)
    whole = jnp.take(jnp.stack(got, 1), order, axis=1)
    whole = whole.reshape(whole.shape[0] * radix, *whole.shape[2:])
    return parted[0], whole


def gathered(y, axis):
    me = lax.axis_index(axis)
    y = y[None]
    for low, radix in reversed(digit_steps(lax.axis_size(axis))):
        mine = (me // low) % radix
        got = [y] + [xor_partner(y, axis, t * low) for t in range(1, radix)]
        order = jnp.bitwise_xor(jnp.arange(radix, dtype=mine.dtype), mine)
        y = jnp.take(jnp.stack(got, 1), order, axis=1)
        y = y.reshape(y.shape[0] * radix, *y.shape[2:])
    return y


def attention_body(pos_ref, q_ref, do_ref, k_ref, v_ref, dk_ref, dv_ref):
    m = pl.program_id(1)
    scale = HEAD_SIZE ** (-0.5)
    q = q_ref[...]
    do = do_ref[...]
    k = k_ref[...]
    v = v_ref[...]
    s = lax.dot_general(q, k, (((1,), (1,)), ((), ())), preferred_element_type=jnp.float32) * scale
    place = lax.broadcasted_iota(jnp.int32, (1, s.shape[1]), 1) // 128
    block = (place % 2) * 4 + ((place // 2) % 2) * 2 + place // 4
    expo = jnp.exp(jnp.where(block <= pos_ref[0], s, -jnp.inf))
    prob = expo * (1.0 / jnp.sum(expo, axis=-1, keepdims=True))
    prob_b = prob.astype(jnp.bfloat16)
    outp = jnp.dot(prob_b, v, preferred_element_type=jnp.float32)
    delta = jnp.sum(do.astype(jnp.float32) * outp, axis=-1, keepdims=True)
    dprob = lax.dot_general(do, v, (((1,), (1,)), ((), ())), preferred_element_type=jnp.float32)
    dscore = (prob * (dprob - delta)).astype(jnp.bfloat16)
    dk = lax.dot_general(dscore, q, (((0,), (0,)), ((), ())), preferred_element_type=jnp.float32)
    dv = lax.dot_general(prob_b, do, (((0,), (0,)), ((), ())), preferred_element_type=jnp.float32)

    @pl.when(m == 0)
    def _():
        dk_ref[...] = dk
        dv_ref[...] = dv

    @pl.when(m > 0)
    def _():
        dk_ref[...] += dk
        dv_ref[...] += dv


def attention_grads(position, queries, out_grad, keys, values):
    tokens = queries.shape[0]
    window_rows, cols = keys.shape
    heads = cols // HEAD_SIZE
    scale = HEAD_SIZE ** (-0.5)
    grid_spec = pltpu.PrefetchScalarGridSpec(
        num_scalar_prefetch=1,
        grid=(heads, Q_PER_KV),
        in_specs=[
            pl.BlockSpec((tokens, HEAD_SIZE), lambda g, m, p: (0, g * Q_PER_KV + m)),
            pl.BlockSpec((tokens, HEAD_SIZE), lambda g, m, p: (0, g * Q_PER_KV + m)),
            pl.BlockSpec((window_rows, HEAD_SIZE), lambda g, m, p: (0, g)),
            pl.BlockSpec((window_rows, HEAD_SIZE), lambda g, m, p: (0, g)),
        ],
        out_specs=[
            pl.BlockSpec((window_rows, HEAD_SIZE), lambda g, m, p: (0, g)),
            pl.BlockSpec((window_rows, HEAD_SIZE), lambda g, m, p: (0, g)),
        ],
    )
    dk, dv = pl.pallas_call(
        attention_body,
        grid_spec=grid_spec,
        out_shape=[jax.ShapeDtypeStruct((window_rows, cols), jnp.float32)] * 2,
        compiler_params=pltpu.CompilerParams(dimension_semantics=("arbitrary", "arbitrary")),
    )(position.reshape(1).astype(jnp.int32), queries, out_grad, keys, values)
    return dk * scale, dv


def on_device(
    file_lengths,
    queries,
    out_grad,
    mem_key,
    memory_values,
    enc_rows,
    key_down,
    key_up,
    value_down,
    value_up,
):
    wide_count = lax.axis_size("wide")
    narrow_count = lax.axis_size("narrow")
    span = 8
    rows = mem_key.shape[0]
    cols = mem_key.shape[1]
    local_heads = cols // HEAD_SIZE
    stretch = lax.axis_index("wide")
    starts = jnp.cumsum(file_lengths) - file_lengths
    first = jnp.max(jnp.where(starts <= stretch, starts, 0))
    position = stretch - first
    window = jnp.stack([mem_key, memory_values])[None]
    reach = span // 2
    while reach >= 1:
        window = jnp.concatenate([window, passed_along(window, "wide", reach)], 0)
        reach //= 2
    keys = window[:, 0].reshape(span * rows, cols)
    values = window[:, 1].reshape(span * rows, cols)
    dkey, dval = attention_grads(position, queries, out_grad, keys, values)
    contrib = jnp.stack([dkey.reshape(span, rows, cols), dval.reshape(span, rows, cols)], 1)
    half = span // 2
    while half >= 1:
        give = contrib[half : 2 * half]
        if half == span // 2:
            give = give.astype(jnp.bfloat16)
        contrib = contrib[:half] + passed_along(give, "wide", -(span // (2 * half))).astype(jnp.float32)
        half //= 2
    total = contrib[0]
    key_grad = total[0].astype(jnp.bfloat16)
    value_grad = total[1].astype(jnp.bfloat16)
    u_key = jnp.dot(enc_rows, key_down, preferred_element_type=jnp.float32).astype(jnp.bfloat16)
    u_value = jnp.dot(enc_rows, value_down, preferred_element_type=jnp.float32).astype(jnp.bfloat16)
    part_key = jnp.dot(key_grad, key_up.T, preferred_element_type=jnp.float32)
    part_value = jnp.dot(value_grad, value_up.T, preferred_element_type=jnp.float32)
    rank = part_key.shape[1]
    piece = rank // narrow_count
    parts = jnp.concatenate(
        [
            part_key.reshape(rows, narrow_count, piece).transpose(1, 0, 2),
            part_value.reshape(rows, narrow_count, piece).transpose(1, 0, 2),
        ],
        2,
    )
    h_both = scattered_sum(parts, "narrow").astype(jnp.bfloat16)
    up_key = jnp.dot(u_key.T, key_grad, preferred_element_type=jnp.float32)
    up_value = jnp.dot(u_value.T, value_grad, preferred_element_type=jnp.float32)
    down = jnp.dot(enc_rows.T, h_both, preferred_element_type=jnp.float32)
    width = down.shape[0] // wide_count
    up_both = jnp.stack([up_key, up_value]).reshape(wide_count, -1)
    down, up_both = wide_sums(down.reshape(wide_count, width * 2 * piece), up_both, "wide")
    down = down.reshape(width, 2, piece)
    up_both = up_both.reshape(2, rank, cols)
    down = gathered(down, "narrow").transpose(1, 2, 0, 3).reshape(width, 2, rank)
    return (down[:, 0], down[:, 1], up_both[0], up_both[1])


def solution(mesh):
    placed = (
        P(),
        P("wide", "narrow"),
        P("wide", "narrow"),
        P("wide", "narrow"),
        P("wide", "narrow"),
        P("wide", None),
        P(),
        P(None, "narrow"),
        P(),
        P(None, "narrow"),
    )
    return jax.shard_map(
        on_device,
        mesh=mesh,
        in_specs=placed,
        out_specs=(P("wide", None), P("wide", None), P(None, "narrow"), P(None, "narrow")),
        check_vma=False,
    )
```

```python
import jax
import jax.numpy as jnp
from jax import lax
from jax.experimental import pallas as pl
from jax.experimental.pallas import tpu as pltpu
from jax.sharding import PartitionSpec as P

HEAD_SIZE = 128
Q_PER_KV = 4


def passed_along(array, axis, by):
    devices = lax.axis_size(axis)
    pairs = [(i, i + by) for i in range(devices) if 0 <= i + by < devices]
    return lax.ppermute(array, axis, pairs)


def digit_steps(devices):
    steps = []
    low = 1
    while low < devices:
        radix = 4 if devices % (low * 4) == 0 else 2
        steps.append((low, radix))
        low *= radix
    return steps


def xor_partner(array, axis, mask):
    devices = lax.axis_size(axis)
    return lax.ppermute(array, axis, [(i, i ^ mask) for i in range(devices)])


def scattered_sum(x, axis, first_kind=None):
    me = lax.axis_index(axis)
    for step, (low, radix) in enumerate(digit_steps(lax.axis_size(axis))):
        group = x.reshape(x.shape[0] // radix, radix, *x.shape[1:])
        mine = (me // low) % radix
        x = lax.dynamic_index_in_dim(group, mine, axis=1, keepdims=False)
        for t in range(1, radix):
            give = lax.dynamic_index_in_dim(group, jnp.bitwise_xor(mine, t), axis=1, keepdims=False)
            if step == 0 and first_kind is not None:
                give = give.astype(first_kind)
            x = x + xor_partner(give, axis, t * low).astype(x.dtype)
    return x[0]


def wide_sums(parted, whole, axis):
    me = lax.axis_index(axis)
    steps = digit_steps(lax.axis_size(axis))
    low, radix = steps[0]
    split = parted.shape[1]
    x = jnp.concatenate([parted, whole], 1)
    group = x.reshape(x.shape[0] // radix, radix, *x.shape[1:])
    first = (me // low) % radix
    x = lax.dynamic_index_in_dim(group, first, axis=1, keepdims=False)
    for t in range(1, radix):
        give = lax.dynamic_index_in_dim(group, jnp.bitwise_xor(first, t), axis=1, keepdims=False)
        x = x + xor_partner(give.astype(jnp.bfloat16), axis, t * low).astype(x.dtype)
    parted = x[:, :split]
    whole = x[:, split:]
    for low, radix in steps[1:]:
        group = parted.reshape(parted.shape[0] // radix, radix, *parted.shape[1:])
        mine = (me // low) % radix
        parted = lax.dynamic_index_in_dim(group, mine, axis=1, keepdims=False)
        size = parted.size
        wholes = [whole]
        for t in range(1, radix):
            give = lax.dynamic_index_in_dim(group, jnp.bitwise_xor(mine, t), axis=1, keepdims=False)
            back = xor_partner(jnp.concatenate([give.reshape(-1), whole.reshape(-1)]), axis, t * low)
            parted = parted + back[:size].reshape(parted.shape)
            wholes.append(back[size:].reshape(whole.shape))
        order = jnp.bitwise_xor(jnp.arange(radix, dtype=mine.dtype), mine)
        ranked = jnp.take(jnp.stack(wholes), order, axis=0)
        whole = ranked[0]
        for d in range(1, radix):
            whole = whole + ranked[d]
    low, radix = steps[0]
    got = [whole] + [xor_partner(whole, axis, t * low) for t in range(1, radix)]
    order = jnp.bitwise_xor(jnp.arange(radix, dtype=first.dtype), first)
    whole = jnp.take(jnp.stack(got, 1), order, axis=1)
    whole = whole.reshape(whole.shape[0] * radix, *whole.shape[2:])
    return parted[0], whole


def gathered(y, axis):
    me = lax.axis_index(axis)
    y = y[None]
    for low, radix in reversed(digit_steps(lax.axis_size(axis))):
        mine = (me // low) % radix
        got = [y] + [xor_partner(y, axis, t * low) for t in range(1, radix)]
        order = jnp.bitwise_xor(jnp.arange(radix, dtype=mine.dtype), mine)
        y = jnp.take(jnp.stack(got, 1), order, axis=1)
        y = y.reshape(y.shape[0] * radix, *y.shape[2:])
    return y


def attention_body(pos_ref, q_ref, do_ref, k_ref, v_ref, dk_ref, dv_ref):
    m = pl.program_id(1)
    scale = HEAD_SIZE ** (-0.5)
    q = q_ref[...]
    do = do_ref[...]
    k = k_ref[...]
    v = v_ref[...]
    s = lax.dot_general(q, k, (((1,), (1,)), ((), ())), preferred_element_type=jnp.float32) * scale
    block = lax.broadcasted_iota(jnp.int32, (1, s.shape[1]), 1) // 128
    expo = jnp.exp(jnp.where(block <= pos_ref[0], s, -jnp.inf))
    prob = expo * (1.0 / jnp.sum(expo, axis=-1, keepdims=True))
    prob_b = prob.astype(jnp.bfloat16)
    outp = jnp.dot(prob_b, v, preferred_element_type=jnp.float32)
    delta = jnp.sum(do.astype(jnp.float32) * outp, axis=-1, keepdims=True)
    dprob = lax.dot_general(do, v, (((1,), (1,)), ((), ())), preferred_element_type=jnp.float32)
    dscore = (prob * (dprob - delta)).astype(jnp.bfloat16)
    dk = lax.dot_general(dscore, q, (((0,), (0,)), ((), ())), preferred_element_type=jnp.float32)
    dv = lax.dot_general(prob_b, do, (((0,), (0,)), ((), ())), preferred_element_type=jnp.float32)

    @pl.when(m == 0)
    def _():
        dk_ref[...] = dk
        dv_ref[...] = dv

    @pl.when(m > 0)
    def _():
        dk_ref[...] += dk
        dv_ref[...] += dv


def attention_grads(position, queries, out_grad, keys, values):
    tokens = queries.shape[0]
    window_rows, cols = keys.shape
    heads = cols // HEAD_SIZE
    scale = HEAD_SIZE ** (-0.5)
    grid_spec = pltpu.PrefetchScalarGridSpec(
        num_scalar_prefetch=1,
        grid=(heads, Q_PER_KV),
        in_specs=[
            pl.BlockSpec((tokens, HEAD_SIZE), lambda g, m, p: (0, g * Q_PER_KV + m)),
            pl.BlockSpec((tokens, HEAD_SIZE), lambda g, m, p: (0, g * Q_PER_KV + m)),
            pl.BlockSpec((window_rows, HEAD_SIZE), lambda g, m, p: (0, g)),
            pl.BlockSpec((window_rows, HEAD_SIZE), lambda g, m, p: (0, g)),
        ],
        out_specs=[
            pl.BlockSpec((window_rows, HEAD_SIZE), lambda g, m, p: (0, g)),
            pl.BlockSpec((window_rows, HEAD_SIZE), lambda g, m, p: (0, g)),
        ],
    )
    dk, dv = pl.pallas_call(
        attention_body,
        grid_spec=grid_spec,
        out_shape=[jax.ShapeDtypeStruct((window_rows, cols), jnp.float32)] * 2,
        compiler_params=pltpu.CompilerParams(dimension_semantics=("arbitrary", "arbitrary")),
    )(position.reshape(1).astype(jnp.int32), queries, out_grad, keys, values)
    return dk * scale, dv


def on_device(
    file_lengths,
    queries,
    out_grad,
    mem_key,
    memory_values,
    enc_rows,
    key_down,
    key_up,
    value_down,
    value_up,
):
    wide_count = lax.axis_size("wide")
    narrow_count = lax.axis_size("narrow")
    span = 8
    rows = mem_key.shape[0]
    cols = mem_key.shape[1]
    local_heads = cols // HEAD_SIZE
    stretch = lax.axis_index("wide")
    starts = jnp.cumsum(file_lengths) - file_lengths
    first = jnp.max(jnp.where(starts <= stretch, starts, 0))
    position = stretch - first
    u_key = jnp.dot(enc_rows, key_down, preferred_element_type=jnp.float32).astype(jnp.bfloat16)
    u_value = jnp.dot(enc_rows, value_down, preferred_element_type=jnp.float32).astype(jnp.bfloat16)
    rank = u_key.shape[1]
    piece = rank // narrow_count
    window = jnp.concatenate([jnp.stack([mem_key, memory_values]), jnp.stack([u_key, u_value])], 2)[None]
    reach = 1
    while reach < span:
        window = jnp.concatenate([window, passed_along(window, "wide", reach)], 0)
        reach *= 2
    keys = window[:, 0, :, :cols].reshape(span * rows, cols)
    values = window[:, 1, :, :cols].reshape(span * rows, cols)
    u_window = window[:, :, :, cols:].astype(jnp.float32)
    dkey, dval = attention_grads(position, queries, out_grad, keys, values)
    dkey = dkey.reshape(span, rows, cols)
    dval = dval.reshape(span, rows, cols)
    exact = lax.Precision.HIGHEST
    up_key = jnp.einsum("jrk,jrc->kc", u_window[:, 0], dkey, precision=exact)
    up_value = jnp.einsum("jrk,jrc->kc", u_window[:, 1], dval, precision=exact)
    part_key = jnp.einsum("jrc,kc->jrk", dkey, key_up.astype(jnp.float32), precision=exact)
    part_value = jnp.einsum("jrc,kc->jrk", dval, value_up.astype(jnp.float32), precision=exact)
    parts = jnp.stack([part_key, part_value], 1).reshape(span, 2, rows, narrow_count, piece)
    contrib = scattered_sum(parts.transpose(3, 0, 1, 2, 4), "narrow")
    reach = span // 2
    while reach >= 1:
        contrib = contrib[:reach] + passed_along(contrib[reach : 2 * reach], "wide", -reach)
        reach //= 2
    total = contrib[0]
    h_both = jnp.concatenate([total[0], total[1]], 1).astype(jnp.bfloat16)
    down = jnp.dot(enc_rows.T, h_both, preferred_element_type=jnp.float32)
    width = down.shape[0] // wide_count
    up_both = jnp.stack([up_key, up_value]).reshape(wide_count, -1)
    down, up_both = wide_sums(down.reshape(wide_count, width * 2 * piece), up_both, "wide")
    down = down.reshape(width, 2, piece)
    up_both = up_both.reshape(2, rank, cols)
    down = gathered(down, "narrow").transpose(1, 2, 0, 3).reshape(width, 2, rank)
    return (down[:, 0], down[:, 1], up_both[0], up_both[1])


def solution(mesh):
    placed = (
        P(),
        P("wide", "narrow"),
        P("wide", "narrow"),
        P("wide", "narrow"),
        P("wide", "narrow"),
        P("wide", None),
        P(),
        P(None, "narrow"),
        P(),
        P(None, "narrow"),
    )
    return jax.shard_map(
        on_device,
        mesh=mesh,
        in_specs=placed,
        out_specs=(P("wide", None), P("wide", None), P(None, "narrow"), P(None, "narrow")),
        check_vma=False,
    )
```

```python
import jax
import jax.numpy as jnp
from jax import lax
from jax.experimental import pallas as pl
from jax.experimental.pallas import tpu as pltpu
from jax.sharding import PartitionSpec as P

HEAD_SIZE = 128
Q_PER_KV = 4


def passed_along(array, axis, by):
    devices = lax.axis_size(axis)
    pairs = [(i, i + by) for i in range(devices) if 0 <= i + by < devices]
    return lax.ppermute(array, axis, pairs)


def digit_steps(devices):
    steps = []
    low = 1
    while low < devices:
        radix = 4 if devices % (low * 4) == 0 else 2
        steps.append((low, radix))
        low *= radix
    return steps


def xor_partner(array, axis, mask):
    devices = lax.axis_size(axis)
    return lax.ppermute(array, axis, [(i, i ^ mask) for i in range(devices)])


def scattered_sum(x, axis, first_kind=None):
    me = lax.axis_index(axis)
    for step, (low, radix) in enumerate(digit_steps(lax.axis_size(axis))):
        group = x.reshape(x.shape[0] // radix, radix, *x.shape[1:])
        mine = (me // low) % radix
        x = lax.dynamic_index_in_dim(group, mine, axis=1, keepdims=False)
        for t in range(1, radix):
            give = lax.dynamic_index_in_dim(group, jnp.bitwise_xor(mine, t), axis=1, keepdims=False)
            if step == 0 and first_kind is not None:
                give = give.astype(first_kind)
            x = x + xor_partner(give, axis, t * low).astype(x.dtype)
    return x[0]


def wide_sums(parted, whole, axis):
    me = lax.axis_index(axis)
    steps = digit_steps(lax.axis_size(axis))
    low, radix = steps[0]
    split = parted.shape[1]
    x = jnp.concatenate([parted, whole], 1)
    group = x.reshape(x.shape[0] // radix, radix, *x.shape[1:])
    first = (me // low) % radix
    x = lax.dynamic_index_in_dim(group, first, axis=1, keepdims=False)
    for t in range(1, radix):
        give = lax.dynamic_index_in_dim(group, jnp.bitwise_xor(first, t), axis=1, keepdims=False)
        x = x + xor_partner(give.astype(jnp.bfloat16), axis, t * low).astype(x.dtype)
    parted = x[:, :split]
    whole = x[:, split:]
    for low, radix in steps[1:]:
        group = parted.reshape(parted.shape[0] // radix, radix, *parted.shape[1:])
        mine = (me // low) % radix
        parted = lax.dynamic_index_in_dim(group, mine, axis=1, keepdims=False)
        size = parted.size
        wholes = [whole]
        for t in range(1, radix):
            give = lax.dynamic_index_in_dim(group, jnp.bitwise_xor(mine, t), axis=1, keepdims=False)
            back = xor_partner(jnp.concatenate([give.reshape(-1), whole.reshape(-1)]), axis, t * low)
            parted = parted + back[:size].reshape(parted.shape)
            wholes.append(back[size:].reshape(whole.shape))
        order = jnp.bitwise_xor(jnp.arange(radix, dtype=mine.dtype), mine)
        ranked = jnp.take(jnp.stack(wholes), order, axis=0)
        whole = ranked[0]
        for d in range(1, radix):
            whole = whole + ranked[d]
    low, radix = steps[0]
    got = [whole] + [xor_partner(whole, axis, t * low) for t in range(1, radix)]
    order = jnp.bitwise_xor(jnp.arange(radix, dtype=first.dtype), first)
    whole = jnp.take(jnp.stack(got, 1), order, axis=1)
    whole = whole.reshape(whole.shape[0] * radix, *whole.shape[2:])
    return parted[0], whole


def gathered(y, axis):
    me = lax.axis_index(axis)
    y = y[None]
    for low, radix in reversed(digit_steps(lax.axis_size(axis))):
        mine = (me // low) % radix
        got = [y] + [xor_partner(y, axis, t * low) for t in range(1, radix)]
        order = jnp.bitwise_xor(jnp.arange(radix, dtype=mine.dtype), mine)
        y = jnp.take(jnp.stack(got, 1), order, axis=1)
        y = y.reshape(y.shape[0] * radix, *y.shape[2:])
    return y


def attention_body(pos_ref, q_ref, do_ref, k_ref, v_ref, dk_ref, dv_ref):
    m = pl.program_id(1)
    scale = HEAD_SIZE ** (-0.5)
    q = q_ref[...]
    do = do_ref[...]
    k = k_ref[...]
    v = v_ref[...]
    s = lax.dot_general(q, k, (((1,), (1,)), ((), ())), preferred_element_type=jnp.float32) * scale
    block = lax.broadcasted_iota(jnp.int32, (1, s.shape[1]), 1) // 128
    expo = jnp.exp(jnp.where(block <= pos_ref[0], s, -jnp.inf))
    prob = expo * (1.0 / jnp.sum(expo, axis=-1, keepdims=True))
    prob_b = prob.astype(jnp.bfloat16)
    outp = jnp.dot(prob_b, v, preferred_element_type=jnp.float32)
    delta = jnp.sum(do.astype(jnp.float32) * outp, axis=-1, keepdims=True)
    dprob = lax.dot_general(do, v, (((1,), (1,)), ((), ())), preferred_element_type=jnp.float32)
    dscore = (prob * (dprob - delta)).astype(jnp.bfloat16)
    dk = lax.dot_general(dscore, q, (((0,), (0,)), ((), ())), preferred_element_type=jnp.float32)
    dv = lax.dot_general(prob_b, do, (((0,), (0,)), ((), ())), preferred_element_type=jnp.float32)

    @pl.when(m == 0)
    def _():
        dk_ref[...] = dk
        dv_ref[...] = dv

    @pl.when(m > 0)
    def _():
        dk_ref[...] += dk
        dv_ref[...] += dv


def attention_grads(position, queries, out_grad, keys, values):
    tokens = queries.shape[0]
    window_rows, cols = keys.shape
    heads = cols // HEAD_SIZE
    scale = HEAD_SIZE ** (-0.5)
    grid_spec = pltpu.PrefetchScalarGridSpec(
        num_scalar_prefetch=1,
        grid=(heads, Q_PER_KV),
        in_specs=[
            pl.BlockSpec((tokens, HEAD_SIZE), lambda g, m, p: (0, g * Q_PER_KV + m)),
            pl.BlockSpec((tokens, HEAD_SIZE), lambda g, m, p: (0, g * Q_PER_KV + m)),
            pl.BlockSpec((window_rows, HEAD_SIZE), lambda g, m, p: (0, g)),
            pl.BlockSpec((window_rows, HEAD_SIZE), lambda g, m, p: (0, g)),
        ],
        out_specs=[
            pl.BlockSpec((window_rows, HEAD_SIZE), lambda g, m, p: (0, g)),
            pl.BlockSpec((window_rows, HEAD_SIZE), lambda g, m, p: (0, g)),
        ],
    )
    dk, dv = pl.pallas_call(
        attention_body,
        grid_spec=grid_spec,
        out_shape=[jax.ShapeDtypeStruct((window_rows, cols), jnp.float32)] * 2,
        compiler_params=pltpu.CompilerParams(dimension_semantics=("arbitrary", "arbitrary")),
    )(position.reshape(1).astype(jnp.int32), queries, out_grad, keys, values)
    return dk * scale, dv


def on_device(
    file_lengths,
    queries,
    out_grad,
    mem_key,
    memory_values,
    enc_rows,
    key_down,
    key_up,
    value_down,
    value_up,
):
    wide_count = lax.axis_size("wide")
    narrow_count = lax.axis_size("narrow")
    span = 8
    rows = mem_key.shape[0]
    cols = mem_key.shape[1]
    local_heads = cols // HEAD_SIZE
    stretch = lax.axis_index("wide")
    starts = jnp.cumsum(file_lengths) - file_lengths
    first = jnp.max(jnp.where(starts <= stretch, starts, 0))
    position = stretch - first
    window = jnp.stack([mem_key, memory_values])[None]
    reach = 1
    while reach < span:
        window = jnp.concatenate([window, passed_along(window, "wide", reach)], 0)
        reach *= 2
    keys = window[:, 0].reshape(span * rows, cols)
    values = window[:, 1].reshape(span * rows, cols)
    dkey, dval = attention_grads(position, queries, out_grad, keys, values)
    contrib = jnp.stack([dkey.reshape(span, rows, cols), dval.reshape(span, rows, cols)], 1)
    reach = span // 2
    while reach >= 1:
        give = contrib[reach : 2 * reach]
        if reach >= span // 4:
            give = give.astype(jnp.bfloat16)
        contrib = contrib[:reach] + passed_along(give, "wide", -reach).astype(jnp.float32)
        reach //= 2
    total = contrib[0]
    key_grad = total[0].astype(jnp.bfloat16)
    value_grad = total[1].astype(jnp.bfloat16)
    u_key = jnp.dot(enc_rows, key_down, preferred_element_type=jnp.float32).astype(jnp.bfloat16)
    u_value = jnp.dot(enc_rows, value_down, preferred_element_type=jnp.float32).astype(jnp.bfloat16)
    part_key = jnp.dot(key_grad, key_up.T, preferred_element_type=jnp.float32)
    part_value = jnp.dot(value_grad, value_up.T, preferred_element_type=jnp.float32)
    rank = part_key.shape[1]
    piece = rank // narrow_count
    parts = jnp.concatenate(
        [
            part_key.reshape(rows, narrow_count, piece).transpose(1, 0, 2),
            part_value.reshape(rows, narrow_count, piece).transpose(1, 0, 2),
        ],
        2,
    )
    h_both = scattered_sum(parts, "narrow").astype(jnp.bfloat16)
    up_key = jnp.dot(u_key.T, key_grad, preferred_element_type=jnp.float32)
    up_value = jnp.dot(u_value.T, value_grad, preferred_element_type=jnp.float32)
    down = jnp.dot(enc_rows.T, h_both, preferred_element_type=jnp.float32)
    width = down.shape[0] // wide_count
    up_both = jnp.stack([up_key, up_value]).reshape(wide_count, -1)
    down, up_both = wide_sums(down.reshape(wide_count, width * 2 * piece), up_both, "wide")
    down = down.reshape(width, 2, piece)
    up_both = up_both.reshape(2, rank, cols)
    down = gathered(down, "narrow").transpose(1, 2, 0, 3).reshape(width, 2, rank)
    return (down[:, 0], down[:, 1], up_both[0], up_both[1])


def solution(mesh):
    placed = (
        P(),
        P("wide", "narrow"),
        P("wide", "narrow"),
        P("wide", "narrow"),
        P("wide", "narrow"),
        P("wide", None),
        P(),
        P(None, "narrow"),
        P(),
        P(None, "narrow"),
    )
    return jax.shard_map(
        on_device,
        mesh=mesh,
        in_specs=placed,
        out_specs=(P("wide", None), P("wide", None), P(None, "narrow"), P(None, "narrow")),
        check_vma=False,
    )
```

```python
import jax
import jax.numpy as jnp
from jax import lax
from jax.experimental import pallas as pl
from jax.experimental.pallas import tpu as pltpu
from jax.sharding import PartitionSpec as P

HEAD_SIZE = 128
Q_PER_KV = 4


def passed_along(array, axis, by):
    devices = lax.axis_size(axis)
    pairs = [(i, i + by) for i in range(devices) if 0 <= i + by < devices]
    return lax.ppermute(array, axis, pairs)


def digit_steps(devices):
    steps = []
    low = 1
    while low < devices:
        radix = 4 if devices % (low * 4) == 0 else 2
        steps.append((low, radix))
        low *= radix
    return steps


def xor_partner(array, axis, mask):
    devices = lax.axis_size(axis)
    return lax.ppermute(array, axis, [(i, i ^ mask) for i in range(devices)])


def scattered_sum(x, axis, first_kind=None):
    me = lax.axis_index(axis)
    for step, (low, radix) in enumerate(digit_steps(lax.axis_size(axis))):
        group = x.reshape(x.shape[0] // radix, radix, *x.shape[1:])
        mine = (me // low) % radix
        x = lax.dynamic_index_in_dim(group, mine, axis=1, keepdims=False)
        for t in range(1, radix):
            give = lax.dynamic_index_in_dim(group, jnp.bitwise_xor(mine, t), axis=1, keepdims=False)
            if step == 0 and first_kind is not None:
                give = give.astype(first_kind)
            x = x + xor_partner(give, axis, t * low).astype(x.dtype)
    return x[0]


def wide_sums(parted, whole, axis):
    me = lax.axis_index(axis)
    steps = digit_steps(lax.axis_size(axis))
    low, radix = steps[0]
    split = parted.shape[1]
    x = jnp.concatenate([parted, whole], 1)
    group = x.reshape(x.shape[0] // radix, radix, *x.shape[1:])
    first = (me // low) % radix
    x = lax.dynamic_index_in_dim(group, first, axis=1, keepdims=False)
    for t in range(1, radix):
        give = lax.dynamic_index_in_dim(group, jnp.bitwise_xor(first, t), axis=1, keepdims=False)
        x = x + xor_partner(give.astype(jnp.bfloat16), axis, t * low).astype(x.dtype)
    parted = x[:, :split]
    whole = x[:, split:]
    for low, radix in steps[1:]:
        group = parted.reshape(parted.shape[0] // radix, radix, *parted.shape[1:])
        mine = (me // low) % radix
        parted = lax.dynamic_index_in_dim(group, mine, axis=1, keepdims=False)
        size = parted.size
        wholes = [whole]
        for t in range(1, radix):
            give = lax.dynamic_index_in_dim(group, jnp.bitwise_xor(mine, t), axis=1, keepdims=False)
            back = xor_partner(jnp.concatenate([give.reshape(-1), whole.reshape(-1)]), axis, t * low)
            parted = parted + back[:size].reshape(parted.shape)
            wholes.append(back[size:].reshape(whole.shape))
        order = jnp.bitwise_xor(jnp.arange(radix, dtype=mine.dtype), mine)
        ranked = jnp.take(jnp.stack(wholes), order, axis=0)
        whole = ranked[0]
        for d in range(1, radix):
            whole = whole + ranked[d]
    low, radix = steps[0]
    got = [whole] + [xor_partner(whole, axis, t * low) for t in range(1, radix)]
    order = jnp.bitwise_xor(jnp.arange(radix, dtype=first.dtype), first)
    whole = jnp.take(jnp.stack(got, 1), order, axis=1)
    whole = whole.reshape(whole.shape[0] * radix, *whole.shape[2:])
    return parted[0], whole


def gathered(y, axis):
    me = lax.axis_index(axis)
    y = y[None]
    for low, radix in reversed(digit_steps(lax.axis_size(axis))):
        mine = (me // low) % radix
        got = [y] + [xor_partner(y, axis, t * low) for t in range(1, radix)]
        order = jnp.bitwise_xor(jnp.arange(radix, dtype=mine.dtype), mine)
        y = jnp.take(jnp.stack(got, 1), order, axis=1)
        y = y.reshape(y.shape[0] * radix, *y.shape[2:])
    return y


def attention_body(pos_ref, q_ref, do_ref, k_ref, v_ref, out_ref):
    m = pl.program_id(1)
    scale = HEAD_SIZE ** (-0.5)
    q = q_ref[...]
    do = do_ref[...]
    k = k_ref[...]
    v = v_ref[...]
    s = lax.dot_general(q, k, (((1,), (1,)), ((), ())), preferred_element_type=jnp.float32) * scale
    block = lax.broadcasted_iota(jnp.int32, (1, s.shape[1]), 1) // 128
    expo = jnp.exp(jnp.where(block <= pos_ref[0], s, -jnp.inf))
    prob = expo * (1.0 / jnp.sum(expo, axis=-1, keepdims=True))
    prob_b = prob.astype(jnp.bfloat16)
    outp = jnp.dot(prob_b, v, preferred_element_type=jnp.float32)
    delta = jnp.sum(do.astype(jnp.float32) * outp, axis=-1, keepdims=True)
    dprob = lax.dot_general(do, v, (((1,), (1,)), ((), ())), preferred_element_type=jnp.float32)
    dscore = (prob * (dprob - delta)).astype(jnp.bfloat16)
    dk = lax.dot_general(dscore, q, (((0,), (0,)), ((), ())), preferred_element_type=jnp.float32)
    dv = lax.dot_general(prob_b, do, (((0,), (0,)), ((), ())), preferred_element_type=jnp.float32)

    blocks, _, rows, width = out_ref.shape
    dk = dk.reshape(blocks, rows, width)
    dv = dv.reshape(blocks, rows, width)

    @pl.when(m == 0)
    def _():
        out_ref[:, 0] = dk
        out_ref[:, 1] = dv

    @pl.when((m > 0) & (m < Q_PER_KV - 1))
    def _():
        out_ref[:, 0] += dk
        out_ref[:, 1] += dv

    @pl.when(m == Q_PER_KV - 1)
    def _():
        out_ref[:, 0] = (out_ref[:, 0] + dk) * scale
        out_ref[:, 1] += dv


def attention_grads(position, queries, out_grad, keys, values, span):
    tokens = queries.shape[0]
    window_rows, cols = keys.shape
    heads = cols // HEAD_SIZE
    rows = window_rows // span
    grid_spec = pltpu.PrefetchScalarGridSpec(
        num_scalar_prefetch=1,
        grid=(heads, Q_PER_KV),
        in_specs=[
            pl.BlockSpec((tokens, HEAD_SIZE), lambda g, m, p: (0, g * Q_PER_KV + m)),
            pl.BlockSpec((tokens, HEAD_SIZE), lambda g, m, p: (0, g * Q_PER_KV + m)),
            pl.BlockSpec((window_rows, HEAD_SIZE), lambda g, m, p: (0, g)),
            pl.BlockSpec((window_rows, HEAD_SIZE), lambda g, m, p: (0, g)),
        ],
        out_specs=pl.BlockSpec((span, 2, rows, HEAD_SIZE), lambda g, m, p: (0, 0, 0, g)),
    )
    return pl.pallas_call(
        attention_body,
        grid_spec=grid_spec,
        out_shape=jax.ShapeDtypeStruct((span, 2, rows, cols), jnp.float32),
        compiler_params=pltpu.CompilerParams(dimension_semantics=("arbitrary", "arbitrary")),
    )(position.reshape(1).astype(jnp.int32), queries, out_grad, keys, values)


def on_device(
    file_lengths,
    queries,
    out_grad,
    mem_key,
    memory_values,
    enc_rows,
    key_down,
    key_up,
    value_down,
    value_up,
):
    wide_count = lax.axis_size("wide")
    narrow_count = lax.axis_size("narrow")
    span = 8
    rows = mem_key.shape[0]
    cols = mem_key.shape[1]
    local_heads = cols // HEAD_SIZE
    stretch = lax.axis_index("wide")
    starts = jnp.cumsum(file_lengths) - file_lengths
    first = jnp.max(jnp.where(starts <= stretch, starts, 0))
    position = stretch - first
    window = jnp.stack([mem_key, memory_values])[None]
    reach = 1
    while reach < span:
        window = jnp.concatenate([window, passed_along(window, "wide", reach)], 0)
        reach *= 2
    keys = window[:, 0].reshape(span * rows, cols)
    values = window[:, 1].reshape(span * rows, cols)
    contrib = attention_grads(position, queries, out_grad, keys, values, span)
    reach = span // 2
    while reach >= 1:
        give = contrib[reach : 2 * reach]
        if reach == span // 2:
            give = give.astype(jnp.bfloat16)
        contrib = contrib[:reach] + passed_along(give, "wide", -reach).astype(jnp.float32)
        reach //= 2
    total = contrib[0]
    key_grad = total[0].astype(jnp.bfloat16)
    value_grad = total[1].astype(jnp.bfloat16)
    u_key = jnp.dot(enc_rows, key_down, preferred_element_type=jnp.float32).astype(jnp.bfloat16)
    u_value = jnp.dot(enc_rows, value_down, preferred_element_type=jnp.float32).astype(jnp.bfloat16)
    part_key = jnp.dot(key_grad, key_up.T, preferred_element_type=jnp.float32)
    part_value = jnp.dot(value_grad, value_up.T, preferred_element_type=jnp.float32)
    rank = part_key.shape[1]
    piece = rank // narrow_count
    parts = jnp.concatenate(
        [
            part_key.reshape(rows, narrow_count, piece).transpose(1, 0, 2),
            part_value.reshape(rows, narrow_count, piece).transpose(1, 0, 2),
        ],
        2,
    )
    h_both = scattered_sum(parts, "narrow").astype(jnp.bfloat16)
    up_key = jnp.dot(u_key.T, key_grad, preferred_element_type=jnp.float32)
    up_value = jnp.dot(u_value.T, value_grad, preferred_element_type=jnp.float32)
    down = jnp.dot(enc_rows.T, h_both, preferred_element_type=jnp.float32)
    width = down.shape[0] // wide_count
    up_both = jnp.stack([up_key, up_value]).reshape(wide_count, -1)
    down, up_both = wide_sums(down.reshape(wide_count, width * 2 * piece), up_both, "wide")
    down = down.reshape(width, 2, piece)
    up_both = up_both.reshape(2, rank, cols)
    down = gathered(down, "narrow").transpose(1, 2, 0, 3).reshape(width, 2, rank)
    return (down[:, 0], down[:, 1], up_both[0], up_both[1])


def solution(mesh):
    placed = (
        P(),
        P("wide", "narrow"),
        P("wide", "narrow"),
        P("wide", "narrow"),
        P("wide", "narrow"),
        P("wide", None),
        P(),
        P(None, "narrow"),
        P(),
        P(None, "narrow"),
    )
    return jax.shard_map(
        on_device,
        mesh=mesh,
        in_specs=placed,
        out_specs=(P("wide", None), P("wide", None), P(None, "narrow"), P(None, "narrow")),
        check_vma=False,
    )
```

```python
import jax
import jax.numpy as jnp
from jax import lax
from jax.experimental import pallas as pl
from jax.experimental.pallas import tpu as pltpu
from jax.sharding import PartitionSpec as P

HEAD_SIZE = 128
Q_PER_KV = 4


def passed_along(array, axis, by):
    devices = lax.axis_size(axis)
    pairs = [(i, i + by) for i in range(devices) if 0 <= i + by < devices]
    return lax.ppermute(array, axis, pairs)


def digit_steps(devices):
    steps = []
    low = 1
    while low < devices:
        radix = 4 if devices % (low * 4) == 0 else 2
        steps.append((low, radix))
        low *= radix
    return steps


def xor_partner(array, axis, mask):
    devices = lax.axis_size(axis)
    return lax.ppermute(array, axis, [(i, i ^ mask) for i in range(devices)])


def scattered_sum(x, axis, first_kind=None):
    me = lax.axis_index(axis)
    for step, (low, radix) in enumerate(digit_steps(lax.axis_size(axis))):
        group = x.reshape(x.shape[0] // radix, radix, *x.shape[1:])
        mine = (me // low) % radix
        x = lax.dynamic_index_in_dim(group, mine, axis=1, keepdims=False)
        for t in range(1, radix):
            give = lax.dynamic_index_in_dim(group, jnp.bitwise_xor(mine, t), axis=1, keepdims=False)
            if step == 0 and first_kind is not None:
                give = give.astype(first_kind)
            x = x + xor_partner(give, axis, t * low).astype(x.dtype)
    return x[0]


def wide_sums(parted, whole, axis):
    me = lax.axis_index(axis)
    steps = digit_steps(lax.axis_size(axis))
    low, radix = steps[0]
    split = parted.shape[1]
    x = jnp.concatenate([parted, whole], 1)
    group = x.reshape(x.shape[0] // radix, radix, *x.shape[1:])
    first = (me // low) % radix
    x = lax.dynamic_index_in_dim(group, first, axis=1, keepdims=False)
    for t in range(1, radix):
        give = lax.dynamic_index_in_dim(group, jnp.bitwise_xor(first, t), axis=1, keepdims=False)
        x = x + xor_partner(give.astype(jnp.bfloat16), axis, t * low).astype(x.dtype)
    parted = x[:, :split]
    whole = x[:, split:]
    for low, radix in steps[1:]:
        group = parted.reshape(parted.shape[0] // radix, radix, *parted.shape[1:])
        mine = (me // low) % radix
        parted = lax.dynamic_index_in_dim(group, mine, axis=1, keepdims=False)
        size = parted.size
        wholes = [whole]
        for t in range(1, radix):
            give = lax.dynamic_index_in_dim(group, jnp.bitwise_xor(mine, t), axis=1, keepdims=False)
            back = xor_partner(jnp.concatenate([give.reshape(-1), whole.reshape(-1)]), axis, t * low)
            parted = parted + back[:size].reshape(parted.shape)
            wholes.append(back[size:].reshape(whole.shape))
        order = jnp.bitwise_xor(jnp.arange(radix, dtype=mine.dtype), mine)
        ranked = jnp.take(jnp.stack(wholes), order, axis=0)
        whole = ranked[0]
        for d in range(1, radix):
            whole = whole + ranked[d]
    low, radix = steps[0]
    got = [whole] + [xor_partner(whole, axis, t * low) for t in range(1, radix)]
    order = jnp.bitwise_xor(jnp.arange(radix, dtype=first.dtype), first)
    whole = jnp.take(jnp.stack(got, 1), order, axis=1)
    whole = whole.reshape(whole.shape[0] * radix, *whole.shape[2:])
    return parted[0], whole


def gathered(y, axis):
    me = lax.axis_index(axis)
    y = y[None]
    for low, radix in reversed(digit_steps(lax.axis_size(axis))):
        mine = (me // low) % radix
        got = [y] + [xor_partner(y, axis, t * low) for t in range(1, radix)]
        order = jnp.bitwise_xor(jnp.arange(radix, dtype=mine.dtype), mine)
        y = jnp.take(jnp.stack(got, 1), order, axis=1)
        y = y.reshape(y.shape[0] * radix, *y.shape[2:])
    return y


def attention_body(pos_ref, q_ref, do_ref, k_ref, v_ref, dk_ref, dv_ref):
    m = pl.program_id(1)
    scale = HEAD_SIZE ** (-0.5)
    q = q_ref[...]
    do = do_ref[...]
    k = k_ref[...]
    v = v_ref[...]
    s = lax.dot_general(q, k, (((1,), (1,)), ((), ())), preferred_element_type=jnp.float32) * scale
    block = lax.broadcasted_iota(jnp.int32, (1, s.shape[1]), 1) // 128
    expo = jnp.exp(jnp.where(block <= pos_ref[0], s, -jnp.inf))
    prob = expo * (1.0 / jnp.sum(expo, axis=-1, keepdims=True))
    prob_b = prob.astype(jnp.bfloat16)
    outp = jnp.dot(prob_b, v, preferred_element_type=jnp.float32)
    delta = jnp.sum(do.astype(jnp.float32) * outp, axis=-1, keepdims=True)
    dprob = lax.dot_general(do, v, (((1,), (1,)), ((), ())), preferred_element_type=jnp.float32)
    dscore = (prob * (dprob - delta)).astype(jnp.bfloat16)
    dk = lax.dot_general(dscore, q, (((0,), (0,)), ((), ())), preferred_element_type=jnp.float32)
    dv = lax.dot_general(prob_b, do, (((0,), (0,)), ((), ())), preferred_element_type=jnp.float32)

    @pl.when(m == 0)
    def _():
        dk_ref[...] = dk
        dv_ref[...] = dv

    @pl.when(m > 0)
    def _():
        dk_ref[...] += dk
        dv_ref[...] += dv


def attention_grads(position, queries, out_grad, keys, values):
    tokens = queries.shape[0]
    window_rows, cols = keys.shape
    heads = cols // HEAD_SIZE
    scale = HEAD_SIZE ** (-0.5)
    grid_spec = pltpu.PrefetchScalarGridSpec(
        num_scalar_prefetch=1,
        grid=(heads, Q_PER_KV),
        in_specs=[
            pl.BlockSpec((tokens, HEAD_SIZE), lambda g, m, p: (0, g * Q_PER_KV + m)),
            pl.BlockSpec((tokens, HEAD_SIZE), lambda g, m, p: (0, g * Q_PER_KV + m)),
            pl.BlockSpec((window_rows, HEAD_SIZE), lambda g, m, p: (0, g)),
            pl.BlockSpec((window_rows, HEAD_SIZE), lambda g, m, p: (0, g)),
        ],
        out_specs=[
            pl.BlockSpec((window_rows, HEAD_SIZE), lambda g, m, p: (0, g)),
            pl.BlockSpec((window_rows, HEAD_SIZE), lambda g, m, p: (0, g)),
        ],
    )
    dk, dv = pl.pallas_call(
        attention_body,
        grid_spec=grid_spec,
        out_shape=[jax.ShapeDtypeStruct((window_rows, cols), jnp.float32)] * 2,
        compiler_params=pltpu.CompilerParams(dimension_semantics=("arbitrary", "arbitrary")),
    )(position.reshape(1).astype(jnp.int32), queries, out_grad, keys, values)
    return dk * scale, dv


def on_device(
    file_lengths,
    queries,
    out_grad,
    mem_key,
    memory_values,
    enc_rows,
    key_down,
    key_up,
    value_down,
    value_up,
):
    wide_count = lax.axis_size("wide")
    narrow_count = lax.axis_size("narrow")
    span = 8
    rows = mem_key.shape[0]
    cols = mem_key.shape[1]
    local_heads = cols // HEAD_SIZE
    stretch = lax.axis_index("wide")
    starts = jnp.cumsum(file_lengths) - file_lengths
    first = jnp.max(jnp.where(starts <= stretch, starts, 0))
    position = stretch - first
    window = jnp.stack([mem_key, memory_values])[None]
    half = span // 2
    window = jnp.concatenate([window] + [passed_along(window, "wide", by) for by in range(1, half)], 0)
    window = jnp.concatenate([window, passed_along(window, "wide", half)], 0)
    keys = window[:, 0].reshape(span * rows, cols)
    values = window[:, 1].reshape(span * rows, cols)
    dkey, dval = attention_grads(position, queries, out_grad, keys, values)
    contrib = jnp.stack([dkey.reshape(span, rows, cols), dval.reshape(span, rows, cols)], 1)
    give = contrib[half:].astype(jnp.bfloat16)
    contrib = contrib[:half] + passed_along(give, "wide", -half).astype(jnp.float32)
    total = contrib[0]
    for by in range(1, half):
        total = total + passed_along(contrib[by], "wide", -by)
    key_grad = total[0].astype(jnp.bfloat16)
    value_grad = total[1].astype(jnp.bfloat16)
    u_key = jnp.dot(enc_rows, key_down, preferred_element_type=jnp.float32).astype(jnp.bfloat16)
    u_value = jnp.dot(enc_rows, value_down, preferred_element_type=jnp.float32).astype(jnp.bfloat16)
    part_key = jnp.dot(key_grad, key_up.T, preferred_element_type=jnp.float32)
    part_value = jnp.dot(value_grad, value_up.T, preferred_element_type=jnp.float32)
    rank = part_key.shape[1]
    piece = rank // narrow_count
    parts = jnp.concatenate(
        [
            part_key.reshape(rows, narrow_count, piece).transpose(1, 0, 2),
            part_value.reshape(rows, narrow_count, piece).transpose(1, 0, 2),
        ],
        2,
    )
    h_both = scattered_sum(parts, "narrow").astype(jnp.bfloat16)
    up_key = jnp.dot(u_key.T, key_grad, preferred_element_type=jnp.float32)
    up_value = jnp.dot(u_value.T, value_grad, preferred_element_type=jnp.float32)
    down = jnp.dot(enc_rows.T, h_both, preferred_element_type=jnp.float32)
    width = down.shape[0] // wide_count
    up_both = jnp.stack([up_key, up_value]).reshape(wide_count, -1)
    down, up_both = wide_sums(down.reshape(wide_count, width * 2 * piece), up_both, "wide")
    down = down.reshape(width, 2, piece)
    up_both = up_both.reshape(2, rank, cols)
    down = gathered(down, "narrow").transpose(1, 2, 0, 3).reshape(width, 2, rank)
    return (down[:, 0], down[:, 1], up_both[0], up_both[1])


def solution(mesh):
    placed = (
        P(),
        P("wide", "narrow"),
        P("wide", "narrow"),
        P("wide", "narrow"),
        P("wide", "narrow"),
        P("wide", None),
        P(),
        P(None, "narrow"),
        P(),
        P(None, "narrow"),
    )
    return jax.shard_map(
        on_device,
        mesh=mesh,
        in_specs=placed,
        out_specs=(P("wide", None), P("wide", None), P(None, "narrow"), P(None, "narrow")),
        check_vma=False,
    )
```

```python
import jax
import jax.numpy as jnp
from jax import lax
from jax.experimental import pallas as pl
from jax.experimental.pallas import tpu as pltpu
from jax.sharding import PartitionSpec as P

HEAD_SIZE = 128
Q_PER_KV = 4


def passed_along(array, axis, by):
    devices = lax.axis_size(axis)
    pairs = [(i, i + by) for i in range(devices) if 0 <= i + by < devices]
    return lax.ppermute(array, axis, pairs)


def digit_steps(devices):
    steps = []
    low = 1
    while low < devices:
        radix = 4 if devices % (low * 4) == 0 and devices > 4 else 2
        steps.append((low, radix))
        low *= radix
    return steps


def xor_partner(array, axis, mask):
    devices = lax.axis_size(axis)
    return lax.ppermute(array, axis, [(i, i ^ mask) for i in range(devices)])


def scattered_sum(x, axis, first_kind=None):
    me = lax.axis_index(axis)
    for step, (low, radix) in enumerate(digit_steps(lax.axis_size(axis))):
        group = x.reshape(x.shape[0] // radix, radix, *x.shape[1:])
        mine = (me // low) % radix
        x = lax.dynamic_index_in_dim(group, mine, axis=1, keepdims=False)
        for t in range(1, radix):
            give = lax.dynamic_index_in_dim(group, jnp.bitwise_xor(mine, t), axis=1, keepdims=False)
            if step == 0 and first_kind is not None:
                give = give.astype(first_kind)
            x = x + xor_partner(give, axis, t * low).astype(x.dtype)
    return x[0]


def wide_sums(parted, whole, axis):
    me = lax.axis_index(axis)
    steps = digit_steps(lax.axis_size(axis))
    low, radix = steps[0]
    split = parted.shape[1]
    x = jnp.concatenate([parted, whole], 1)
    group = x.reshape(x.shape[0] // radix, radix, *x.shape[1:])
    first = (me // low) % radix
    x = lax.dynamic_index_in_dim(group, first, axis=1, keepdims=False)
    for t in range(1, radix):
        give = lax.dynamic_index_in_dim(group, jnp.bitwise_xor(first, t), axis=1, keepdims=False)
        x = x + xor_partner(give.astype(jnp.bfloat16), axis, t * low).astype(x.dtype)
    parted = x[:, :split]
    whole = x[:, split:]
    for low, radix in steps[1:]:
        group = parted.reshape(parted.shape[0] // radix, radix, *parted.shape[1:])
        mine = (me // low) % radix
        parted = lax.dynamic_index_in_dim(group, mine, axis=1, keepdims=False)
        size = parted.size
        wholes = [whole]
        for t in range(1, radix):
            give = lax.dynamic_index_in_dim(group, jnp.bitwise_xor(mine, t), axis=1, keepdims=False)
            back = xor_partner(jnp.concatenate([give.reshape(-1), whole.reshape(-1)]), axis, t * low)
            parted = parted + back[:size].reshape(parted.shape)
            wholes.append(back[size:].reshape(whole.shape))
        order = jnp.bitwise_xor(jnp.arange(radix, dtype=mine.dtype), mine)
        ranked = jnp.take(jnp.stack(wholes), order, axis=0)
        whole = ranked[0]
        for d in range(1, radix):
            whole = whole + ranked[d]
    low, radix = steps[0]
    got = [whole] + [xor_partner(whole, axis, t * low) for t in range(1, radix)]
    order = jnp.bitwise_xor(jnp.arange(radix, dtype=first.dtype), first)
    whole = jnp.take(jnp.stack(got, 1), order, axis=1)
    whole = whole.reshape(whole.shape[0] * radix, *whole.shape[2:])
    return parted[0], whole


def gathered(y, axis):
    me = lax.axis_index(axis)
    y = y[None]
    for low, radix in reversed(digit_steps(lax.axis_size(axis))):
        mine = (me // low) % radix
        got = [y] + [xor_partner(y, axis, t * low) for t in range(1, radix)]
        order = jnp.bitwise_xor(jnp.arange(radix, dtype=mine.dtype), mine)
        y = jnp.take(jnp.stack(got, 1), order, axis=1)
        y = y.reshape(y.shape[0] * radix, *y.shape[2:])
    return y


def attention_body(pos_ref, q_ref, do_ref, k_ref, v_ref, dk_ref, dv_ref):
    m = pl.program_id(1)
    scale = HEAD_SIZE ** (-0.5)
    q = q_ref[...]
    do = do_ref[...]
    k = k_ref[...]
    v = v_ref[...]
    s = lax.dot_general(q, k, (((1,), (1,)), ((), ())), preferred_element_type=jnp.float32) * scale
    block = lax.broadcasted_iota(jnp.int32, (1, s.shape[1]), 1) // 128
    expo = jnp.exp(jnp.where(block <= pos_ref[0], s, -jnp.inf))
    prob = expo * (1.0 / jnp.sum(expo, axis=-1, keepdims=True))
    prob_b = prob.astype(jnp.bfloat16)
    outp = jnp.dot(prob_b, v, preferred_element_type=jnp.float32)
    delta = jnp.sum(do.astype(jnp.float32) * outp, axis=-1, keepdims=True)
    dprob = lax.dot_general(do, v, (((1,), (1,)), ((), ())), preferred_element_type=jnp.float32)
    dscore = (prob * (dprob - delta)).astype(jnp.bfloat16)
    dk = lax.dot_general(dscore, q, (((0,), (0,)), ((), ())), preferred_element_type=jnp.float32)
    dv = lax.dot_general(prob_b, do, (((0,), (0,)), ((), ())), preferred_element_type=jnp.float32)

    @pl.when(m == 0)
    def _():
        dk_ref[...] = dk
        dv_ref[...] = dv

    @pl.when(m > 0)
    def _():
        dk_ref[...] += dk
        dv_ref[...] += dv


def attention_grads(position, queries, out_grad, keys, values):
    tokens = queries.shape[0]
    window_rows, cols = keys.shape
    heads = cols // HEAD_SIZE
    scale = HEAD_SIZE ** (-0.5)
    grid_spec = pltpu.PrefetchScalarGridSpec(
        num_scalar_prefetch=1,
        grid=(heads, Q_PER_KV),
        in_specs=[
            pl.BlockSpec((tokens, HEAD_SIZE), lambda g, m, p: (0, g * Q_PER_KV + m)),
            pl.BlockSpec((tokens, HEAD_SIZE), lambda g, m, p: (0, g * Q_PER_KV + m)),
            pl.BlockSpec((window_rows, HEAD_SIZE), lambda g, m, p: (0, g)),
            pl.BlockSpec((window_rows, HEAD_SIZE), lambda g, m, p: (0, g)),
        ],
        out_specs=[
            pl.BlockSpec((window_rows, HEAD_SIZE), lambda g, m, p: (0, g)),
            pl.BlockSpec((window_rows, HEAD_SIZE), lambda g, m, p: (0, g)),
        ],
    )
    dk, dv = pl.pallas_call(
        attention_body,
        grid_spec=grid_spec,
        out_shape=[jax.ShapeDtypeStruct((window_rows, cols), jnp.float32)] * 2,
        compiler_params=pltpu.CompilerParams(dimension_semantics=("arbitrary", "arbitrary")),
    )(position.reshape(1).astype(jnp.int32), queries, out_grad, keys, values)
    return dk * scale, dv


def on_device(
    file_lengths,
    queries,
    out_grad,
    mem_key,
    memory_values,
    enc_rows,
    key_down,
    key_up,
    value_down,
    value_up,
):
    wide_count = lax.axis_size("wide")
    narrow_count = lax.axis_size("narrow")
    span = 8
    rows = mem_key.shape[0]
    cols = mem_key.shape[1]
    local_heads = cols // HEAD_SIZE
    stretch = lax.axis_index("wide")
    starts = jnp.cumsum(file_lengths) - file_lengths
    first = jnp.max(jnp.where(starts <= stretch, starts, 0))
    position = stretch - first
    window = jnp.stack([mem_key, memory_values])[None]
    reach = 1
    while reach < span:
        window = jnp.concatenate([window, passed_along(window, "wide", reach)], 0)
        reach *= 2
    keys = window[:, 0].reshape(span * rows, cols)
    values = window[:, 1].reshape(span * rows, cols)
    dkey, dval = attention_grads(position, queries, out_grad, keys, values)
    contrib = jnp.stack([dkey.reshape(span, rows, cols), dval.reshape(span, rows, cols)], 1)
    reach = span // 2
    while reach >= 1:
        give = contrib[reach : 2 * reach]
        if reach == span // 2:
            give = give.astype(jnp.bfloat16)
        contrib = contrib[:reach] + passed_along(give, "wide", -reach).astype(jnp.float32)
        reach //= 2
    total = contrib[0]
    key_grad = total[0].astype(jnp.bfloat16)
    value_grad = total[1].astype(jnp.bfloat16)
    u_key = jnp.dot(enc_rows, key_down, preferred_element_type=jnp.float32).astype(jnp.bfloat16)
    u_value = jnp.dot(enc_rows, value_down, preferred_element_type=jnp.float32).astype(jnp.bfloat16)
    part_key = jnp.dot(key_grad, key_up.T, preferred_element_type=jnp.float32)
    part_value = jnp.dot(value_grad, value_up.T, preferred_element_type=jnp.float32)
    rank = part_key.shape[1]
    piece = rank // narrow_count
    parts = jnp.concatenate(
        [
            part_key.reshape(rows, narrow_count, piece).transpose(1, 0, 2),
            part_value.reshape(rows, narrow_count, piece).transpose(1, 0, 2),
        ],
        2,
    )
    h_both = scattered_sum(parts, "narrow").astype(jnp.bfloat16)
    up_key = jnp.dot(u_key.T, key_grad, preferred_element_type=jnp.float32)
    up_value = jnp.dot(u_value.T, value_grad, preferred_element_type=jnp.float32)
    down = jnp.dot(enc_rows.T, h_both, preferred_element_type=jnp.float32)
    width = down.shape[0] // wide_count
    up_both = jnp.stack([up_key, up_value]).reshape(wide_count, -1)
    down, up_both = wide_sums(down.reshape(wide_count, width * 2 * piece), up_both, "wide")
    down = down.reshape(width, 2, piece)
    up_both = up_both.reshape(2, rank, cols)
    down = gathered(down, "narrow").transpose(1, 2, 0, 3).reshape(width, 2, rank)
    return (down[:, 0], down[:, 1], up_both[0], up_both[1])


def solution(mesh):
    placed = (
        P(),
        P("wide", "narrow"),
        P("wide", "narrow"),
        P("wide", "narrow"),
        P("wide", "narrow"),
        P("wide", None),
        P(),
        P(None, "narrow"),
        P(),
        P(None, "narrow"),
    )
    return jax.shard_map(
        on_device,
        mesh=mesh,
        in_specs=placed,
        out_specs=(P("wide", None), P("wide", None), P(None, "narrow"), P(None, "narrow")),
        check_vma=False,
    )
```
